512 devices in a mesh: req: 64 (over x, z, core), tp: 8 (over y).
Axes of the slice: x: 4, y: 8, z: 8, core: 2. Of those that a mesh axis runs over, the one named last changes fastest.
Arguments:
- dec_q: bfloat16 [8192, 3072], P('req', 'tp'), may hold values from -12 to 12
- dec_kv: bfloat16 [8192, 2048], P('req', 'tp'), may hold values from -12 to 12
- dec_owner: int32 [8192], P('req'), may hold values from 0 to 63, as said below
- dec_table: int32 [16384, 2], P('req'), may hold values from 0 to 512, as said below
- pre_q: bfloat16 [16384, 3072], P('req', 'tp'), may hold values from -12 to 12
- pre_kv: bfloat16 [16384, 2048], P('req', 'tp'), may hold values from -12 to 12
- pre_meta: int32 [64, 3], P('req'), may hold values from 0 to 512, as said below
- pool: bfloat16 [32768, 2048], P('req', 'tp'), may hold values from -12 to 12
- wo: bfloat16 [3072, 3072], P('tp'), may hold values from -0.4375 to 0.4375
Outputs:
- dec_out: bfloat16 [8192, 3072], P(('req', 'tp'))
- pre_out: bfloat16 [16384, 3072], P(('req', 'tp'))
The draws below stay inside these ranges and needn't reach their ends.
Inputs may be any that keep to these rules, and one draw needn't show every extreme that they name: `dec_owner`: among the decode tokens of one group at most 4 name the same owner; in every draw some group is named by exactly 4 tokens of every group. `dec_table`: row o * 256 + s * 4 + c describes the c-th decode token of group s (in row order) that names owner o: start and length of its cache in o's pool, length at least 1, start + length <= 512; rows with no such token hold 0 0. Some window has length 512. `pre_meta`: start + context length <= 512; span length from 64 to 256; some group has context length 512, some span length 256.
All inputs are finite; a program needn't handle non-finite values.
Results may differ from the reference program's by a relative error of at most 0.014.
Values may be sent and summed in bfloat16 or wider, within the bound.
No kernel may reach another device: no remote copies, remote signals or barrier semaphores. Data moves between devices by JAX's collectives and lax.ppermute only.
A program may use at most 64 MiB of HBM per device.

```python
import math
import jax
import jax.numpy as jnp
from jax import lax

D = 3072
HEADS = 24
KVH = 8
HD = 128
TOK_DEV = 128
SPAN = 256
POOL = 512
QPK = 3
GROUPS = 64
CAP = 4
SLOTS = 256
DEC = 8192
PRE = 16384
N_REQ = 64
N_TP = 8


def route_plan(key):
    base_key = jax.random.fold_in(key, 11)
    target = jax.random.randint(jax.random.fold_in(base_key, 1), (), 0, GROUPS).astype(jnp.int32)

    def one_source(source_key):
        first_key, second_key = jax.random.split(source_key)
        shuffled = jax.random.permutation(first_key, (GROUPS - 1) * CAP)[:TOK_DEV - CAP].astype(jnp.int32)
        others = shuffled // CAP
        others = others + (others >= target).astype(jnp.int32)
        destinations = jnp.concatenate([jnp.zeros((CAP,), jnp.int32) + target, others])
        return destinations[jax.random.permutation(second_key, TOK_DEV)]
    owners = jax.vmap(one_source)(jax.random.split(jax.random.fold_in(base_key, 2), GROUPS))
    hot_table = (owners[:, :, None] == jnp.arange(GROUPS, dtype=jnp.int32)[None, None, :]).astype(jnp.int32)
    ranking = jnp.sum((jnp.cumsum(hot_table, axis=1) - hot_table) * hot_table, axis=2)
    sources = jnp.broadcast_to(jnp.arange(GROUPS, dtype=jnp.int32)[:, None], (GROUPS, TOK_DEV))
    filled = jnp.zeros((GROUPS, GROUPS, CAP), jnp.int32).at[owners, sources, ranking].set(1)
    grid_shape = (GROUPS, GROUPS, CAP)
    divisor = jax.random.randint(jax.random.fold_in(base_key, 3), grid_shape, 1, 9)
    longest = jnp.maximum(POOL // divisor, 1)
    jitter = jax.random.randint(jax.random.fold_in(base_key, 4), grid_shape, 0, longest // 2 + 1)
    lengths = longest - jitter
    begins = jax.random.randint(jax.random.fold_in(base_key, 5), grid_shape, 0, POOL - lengths + 1)
    marked = jnp.arange(3, dtype=jnp.int32)
    lengths = lengths.at[target, marked, 0].set(POOL - marked)
    begins = begins.at[target, marked, 0].set(marked)
    row_table = jnp.stack([begins * filled, lengths * filled], axis=-1).reshape(GROUPS * SLOTS, 2).astype(jnp.int32)
    return (owners.reshape(DEC).astype(jnp.int32), row_table)


def prefill_plan(key):
    base_key = jax.random.fold_in(key, 41)
    begins = jax.random.randint(jax.random.fold_in(base_key, 1), (GROUPS,), 0, POOL + 1)
    context = jax.random.randint(jax.random.fold_in(base_key, 2), (GROUPS,), 0, POOL - begins + 1)
    widest = jax.random.randint(jax.random.fold_in(base_key, 3), (), 0, GROUPS)
    begins = begins.at[widest].set(0)
    context = context.at[widest].set(POOL)
    span_len = jax.random.randint(jax.random.fold_in(base_key, 4), (GROUPS,), SPAN // 4, SPAN + 1)
    fullest = jax.random.randint(jax.random.fold_in(base_key, 5), (), 0, GROUPS)
    span_len = span_len.at[fullest].set(SPAN)
    return jnp.stack([begins, context, span_len], axis=1).astype(jnp.int32)


def query_noise(key, row_count):
    return 1.4 * jax.random.truncated_normal(key, -4.0, 4.0, (row_count, HEADS * HD), jnp.float32)


def kv_noise(key, row_count):
    values = jax.random.truncated_normal(key, -4.0, 4.0, (row_count, KVH, 2, HD), jnp.float32)
    return values * jnp.array([1.4, 1.0], jnp.float32)[None, None, :, None]


def draw_dec_owner(key, part):
    return route_plan(key)[0]


def draw_dec_table(key, part):
    return route_plan(key)[1]


def draw_pre_meta(key, part):
    return prefill_plan(key)


def draw_dec_q(key, part):
    values = query_noise(jax.random.fold_in(key, 21), DEC)
    return values.astype(jnp.bfloat16)


def draw_dec_kv(key, part):
    values = kv_noise(jax.random.fold_in(key, 22), DEC)
    return values.reshape(DEC, KVH * 2 * HD).astype(jnp.bfloat16)


def draw_pool(key, part):
    pool_rows = GROUPS * POOL
    values = kv_noise(jax.random.fold_in(key, 23), pool_rows)
    return values.reshape(pool_rows, KVH * 2 * HD).astype(jnp.bfloat16)


def draw_pre_q(key, part):
    values = query_noise(jax.random.fold_in(key, 25), PRE)
    return values.astype(jnp.bfloat16)


def draw_pre_kv(key, part):
    values = kv_noise(jax.random.fold_in(key, 26), PRE)
    return values.reshape(PRE, KVH * 2 * HD).astype(jnp.bfloat16)


def shard_levels(key, shape, cuts, low, largest):
    factor_of, own = 1.0, jax.random.fold_in(key, 6)
    for axis_at, blocks in cuts:
        draws = jnp.exp(jax.random.uniform(jax.random.fold_in(own, axis_at), (blocks,), jnp.float32, low / len(cuts), largest / len(cuts)))
        factor_of = factor_of * jnp.repeat(draws, shape[axis_at] // blocks).reshape([-1 if axis == axis_at else 1 for axis in range(len(shape))])
    return factor_of


def centred(rng, shape, width, limit, cuts=(), kind=jnp.bfloat16):
    entries = jax.random.normal(rng, shape, jnp.float32) * width
    if len(cuts) > 0:
        entries = shard_levels(rng, shape, cuts, -0.22, 0.18) * entries
    return jnp.clip(entries, min=-limit, max=limit).astype(kind)


def setup_inputs(seed: int = 0) -> dict:
    splits = jax.random.split(jax.random.key(seed), 10)
    return {
        "dec_q": draw_dec_q(jax.random.fold_in(splits[9], 71), 0),
        "dec_kv": draw_dec_kv(jax.random.fold_in(splits[9], 71), 0),
        "dec_owner": draw_dec_owner(jax.random.fold_in(splits[9], 71), 0),
        "dec_table": draw_dec_table(jax.random.fold_in(splits[9], 71), 0),
        "pre_q": draw_pre_q(jax.random.fold_in(splits[9], 71), 0),
        "pre_kv": draw_pre_kv(jax.random.fold_in(splits[9], 71), 0),
        "pre_meta": draw_pre_meta(jax.random.fold_in(splits[9], 71), 0),
        "pool": draw_pool(jax.random.fold_in(splits[9], 71), 0),
        "wo": centred(splits[8], (HEADS * HD, D), (D // 16) ** -0.5, 0.4375, ((0, 8),)),
    }


MASKED_SCORE = -1e+30

def rounded_copy(values):
    return lax.optimization_barrier(values.astype(jnp.bfloat16)).astype(jnp.float32)

def decode_group(q_slots, kv_slots, cache_rows, windows):
    score_scale = 1.0 / math.sqrt(HD)
    queries = q_slots.astype(jnp.float32).reshape(SLOTS, KVH, QPK, HD)
    own_kv = kv_slots.astype(jnp.float32).reshape(SLOTS, KVH, 2, HD)
    cached = cache_rows.astype(jnp.float32).reshape(POOL, KVH, 2, HD)
    places = jnp.arange(POOL, dtype=jnp.int32)
    begins = windows[:, 0:1]
    visible = (places[None, :] >= begins) & (places[None, :] < begins + windows[:, 1:2])
    visible = visible[:, None, None, :]
    pool_scores = jnp.einsum('sghd,pgd->sghp', queries, cached[:, :, 0, :]) * score_scale
    pool_scores = jnp.where(visible, pool_scores, MASKED_SCORE)
    self_scores = jnp.einsum('sghd,sgd->sgh', queries, own_kv[:, :, 0, :]) * score_scale
    row_peak = jnp.maximum(lax.optimization_barrier(jnp.max(pool_scores, axis=-1)), self_scores)
    pool_exp = jnp.where(visible, jnp.exp(pool_scores - row_peak[..., None]), 0.0)
    self_exp = jnp.exp(self_scores - row_peak)
    row_total = lax.optimization_barrier(jnp.sum(pool_exp, axis=-1)) + self_exp
    pool_weight = rounded_copy(pool_exp / row_total[..., None])
    self_weight = rounded_copy(self_exp / row_total)
    mixed_rows = jnp.einsum('sghp,pgd->sghd', pool_weight, cached[:, :, 1, :])
    mixed_rows = mixed_rows + self_weight[..., None] * own_kv[:, :, None, 1, :]
    return mixed_rows.astype(jnp.bfloat16).reshape(SLOTS, HEADS * HD)

def prefill_group(q_rows, kv_rows, cache_rows, meta_row):
    score_scale = 1.0 / math.sqrt(HD)
    queries = q_rows.astype(jnp.float32).reshape(SPAN, KVH, QPK, HD)
    span_kv = kv_rows.astype(jnp.float32).reshape(SPAN, KVH, 2, HD)
    cached = cache_rows.astype(jnp.float32).reshape(POOL, KVH, 2, HD)
    places = jnp.arange(POOL, dtype=jnp.int32)
    visible = (places >= meta_row[0]) & (places < meta_row[0] + meta_row[1])
    visible = visible[None, None, None, :]
    row_iota = jnp.arange(SPAN, dtype=jnp.int32)
    causal = (row_iota[None, :] <= row_iota[:, None])[:, None, None, :]
    pool_scores = jnp.einsum('jghd,pgd->jghp', queries, cached[:, :, 0, :]) * score_scale
    pool_scores = jnp.where(visible, pool_scores, MASKED_SCORE)
    span_scores = jnp.einsum('jghd,igd->jghi', queries, span_kv[:, :, 0, :]) * score_scale
    span_scores = jnp.where(causal, span_scores, MASKED_SCORE)
    row_peak = jnp.maximum(lax.optimization_barrier(jnp.max(pool_scores, axis=-1)), lax.optimization_barrier(jnp.max(span_scores, axis=-1)))
    pool_exp = jnp.where(visible, jnp.exp(pool_scores - row_peak[..., None]), 0.0)
    span_exp = jnp.where(causal, jnp.exp(span_scores - row_peak[..., None]), 0.0)
    row_total = lax.optimization_barrier(jnp.sum(pool_exp, axis=-1)) + lax.optimization_barrier(jnp.sum(span_exp, axis=-1))
    pool_weight = rounded_copy(pool_exp / row_total[..., None])
    span_weight = rounded_copy(span_exp / row_total[..., None])
    mixed_rows = jnp.einsum('jghp,pgd->jghd', pool_weight, cached[:, :, 1, :])
    mixed_rows = mixed_rows + jnp.einsum('jghi,igd->jghd', span_weight, span_kv[:, :, 1, :])
    live = (row_iota < meta_row[2])[:, None, None, None]
    return jnp.where(live, mixed_rows, 0.0).astype(jnp.bfloat16).reshape(SPAN, HEADS * HD)

def project(attn_rows, wo):
    shard_width = HEADS * HD // N_TP
    summed = jnp.zeros((attn_rows.shape[0], D), jnp.float32)
    for tp_index in range(N_TP):
        lower = tp_index * shard_width
        partial_term = jnp.dot(attn_rows[:, lower:lower + shard_width], wo[lower:lower + shard_width], preferred_element_type=jnp.float32)
        summed = summed + rounded_copy(partial_term)
    return summed.astype(jnp.bfloat16)

def reference(dec_q, dec_kv, dec_owner, dec_table, pre_q, pre_kv, pre_meta, pool, wo):
    owners = dec_owner.reshape(N_REQ, TOK_DEV)
    hot_table = (owners[:, :, None] == jnp.arange(N_REQ, dtype=jnp.int32)[None, None, :]).astype(jnp.int32)
    ranking = lax.optimization_barrier(jnp.sum((jnp.cumsum(hot_table, axis=1) - hot_table) * hot_table, axis=2))
    sources = jnp.broadcast_to(jnp.arange(N_REQ, dtype=jnp.int32)[:, None], (N_REQ, TOK_DEV))
    slot_ids = (owners * SLOTS + sources * CAP + ranking).reshape(DEC).astype(jnp.int32)
    row_of_slot = jnp.full((N_REQ * SLOTS,), DEC, jnp.int32).at[slot_ids].set(jnp.arange(DEC, dtype=jnp.int32))
    q_padded = jnp.concatenate([dec_q, jnp.zeros((1, HEADS * HD), dec_q.dtype)], axis=0)
    kv_padded = jnp.concatenate([dec_kv, jnp.zeros((1, KVH * 2 * HD), dec_kv.dtype)], axis=0)
    pool_groups = pool.reshape(N_REQ, POOL, KVH * 2 * HD)

    def per_owner(pieces):
        picks = pieces[0]
        return decode_group(q_padded[picks], kv_padded[picks], pieces[1], pieces[2])
    slot_attn = lax.map(per_owner, (row_of_slot.reshape(N_REQ, SLOTS), pool_groups, dec_table.reshape(N_REQ, SLOTS, 2)))
    dec_attn = slot_attn.reshape(N_REQ * SLOTS, HEADS * HD)[slot_ids]

    def per_group(pieces):
        return prefill_group(pieces[0], pieces[1], pieces[2], pieces[3])
    pre_attn = lax.map(per_group, (pre_q.reshape(N_REQ, SPAN, HEADS * HD), pre_kv.reshape(N_REQ, SPAN, KVH * 2 * HD), pool_groups, pre_meta))
    pre_attn = pre_attn.reshape(PRE, HEADS * HD)
    return (project(dec_attn, wo), project(pre_attn, wo))
```

```python
import math

import jax
import jax.numpy as jnp
from jax import lax
from jax.sharding import PartitionSpec as P

HD = 128
QPK = 3


MASKED_SCORE = -1e30


def decode_block(q_block, kv_block, windows, pool_keys, pool_vals):
    score_scale = 1.0 / math.sqrt(HD)
    slot_rows = q_block.shape[0]
    places = lax.iota(jnp.int32, pool_keys.shape[0])
    begins = windows[:, 0:1]
    visible = (places[None, :] >= begins) & (places[None, :] < begins + windows[:, 1:2])
    visible = visible[:, None, None, :]
    pool_scores = (
        jnp.einsum("sghd,pgd->sghp", q_block, pool_keys, preferred_element_type=jnp.float32)
        * score_scale
    )
    pool_scores = jnp.where(visible, pool_scores, MASKED_SCORE)
    self_scores = (
        jnp.einsum(
            "sghd,sgd->sgh", q_block, kv_block[:, :, 0, :], preferred_element_type=jnp.float32
        )
        * score_scale
    )
    row_peak = jnp.maximum(jnp.max(pool_scores, axis=-1), self_scores)
    pool_exp = jnp.where(visible, jnp.exp(pool_scores - row_peak[..., None]), 0.0)
    self_exp = jnp.exp(self_scores - row_peak)
    row_total = jnp.sum(pool_exp, axis=-1) + self_exp
    pool_weight = (pool_exp / row_total[..., None]).astype(jnp.bfloat16)
    self_weight = (self_exp / row_total).astype(jnp.bfloat16)
    mixed_rows = jnp.einsum(
        "sghp,pgd->sghd", pool_weight, pool_vals, preferred_element_type=jnp.float32
    )
    mixed_rows = mixed_rows + self_weight.astype(jnp.float32)[..., None] * kv_block[
        :, :, None, 1, :
    ].astype(jnp.float32)
    return mixed_rows.astype(jnp.bfloat16).reshape(slot_rows, -1)


def prefill_attend(q_rows, kv_rows, meta_row, pool_keys, pool_vals, kv_heads):
    score_scale = 1.0 / math.sqrt(HD)
    span_rows = q_rows.shape[0]
    queries = q_rows.reshape(span_rows, kv_heads, QPK, HD)
    span_kv = kv_rows.reshape(span_rows, kv_heads, 2, HD)
    places = lax.iota(jnp.int32, pool_keys.shape[0])
    visible = (places >= meta_row[0]) & (places < meta_row[0] + meta_row[1])
    visible = visible[None, None, None, :]
    row_iota = lax.iota(jnp.int32, span_rows)
    causal = (row_iota[None, :] <= row_iota[:, None])[:, None, None, :]
    pool_scores = (
        jnp.einsum("jghd,pgd->jghp", queries, pool_keys, preferred_element_type=jnp.float32)
        * score_scale
    )
    pool_scores = jnp.where(visible, pool_scores, MASKED_SCORE)
    span_scores = (
        jnp.einsum(
            "jghd,igd->jghi", queries, span_kv[:, :, 0, :], preferred_element_type=jnp.float32
        )
        * score_scale
    )
    span_scores = jnp.where(causal, span_scores, MASKED_SCORE)
    row_peak = jnp.maximum(jnp.max(pool_scores, axis=-1), jnp.max(span_scores, axis=-1))
    pool_exp = jnp.where(visible, jnp.exp(pool_scores - row_peak[..., None]), 0.0)
    span_exp = jnp.where(causal, jnp.exp(span_scores - row_peak[..., None]), 0.0)
    row_total = jnp.sum(pool_exp, axis=-1) + jnp.sum(span_exp, axis=-1)
    pool_weight = (pool_exp / row_total[..., None]).astype(jnp.bfloat16)
    span_weight = (span_exp / row_total[..., None]).astype(jnp.bfloat16)
    mixed_rows = jnp.einsum(
        "jghp,pgd->jghd", pool_weight, pool_vals, preferred_element_type=jnp.float32
    )
    mixed_rows = mixed_rows + jnp.einsum(
        "jghi,igd->jghd", span_weight, span_kv[:, :, 1, :], preferred_element_type=jnp.float32
    )
    live = (row_iota < meta_row[2])[:, None, None, None]
    return jnp.where(live, mixed_rows, 0.0).astype(jnp.bfloat16).reshape(span_rows, -1)


def term_maker(rows_source, wo):
    return jnp.dot(rows_source, wo, preferred_element_type=jnp.float32)


def per_device(dec_q, dec_kv, dec_owner, dec_table, pre_q, pre_kv, pre_meta, pool, wo):
    groups = lax.axis_size("req")
    tok_rows = dec_q.shape[0]
    capacity = max(2, (2 * tok_rows + groups - 1) // groups)
    slot_count = groups * capacity
    q_width = dec_q.shape[1]
    kv_width = dec_kv.shape[1]
    kv_heads = pool.shape[1] // (2 * HD)
    pool_rows = pool.reshape(pool.shape[0], kv_heads, 2, HD)
    pool_keys = pool_rows[:, :, 0, :]
    pool_vals = pool_rows[:, :, 1, :]

    pre_attn = prefill_attend(pre_q, pre_kv, pre_meta[0], pool_keys, pool_vals, kv_heads)
    pre_part = term_maker(pre_attn, wo).astype(jnp.bfloat16)

    group_iota = lax.iota(jnp.int32, groups)
    hot_table = (dec_owner[:, None] == group_iota[None, :]).astype(jnp.int32)
    ranking = jnp.sum((jnp.cumsum(hot_table, axis=0) - hot_table) * hot_table, axis=1)
    slot_ids = dec_owner * capacity + ranking
    dispatch = (slot_ids[None, :] == lax.iota(jnp.int32, slot_count)[:, None]).astype(jnp.bfloat16)
    send = (
        jnp.dot(dispatch, jnp.concatenate([dec_q, dec_kv], axis=1), preferred_element_type=jnp.float32)
        .astype(jnp.bfloat16)
        .reshape(groups, capacity, q_width + kv_width)
    )
    recv = lax.all_to_all(send, "req", split_axis=0, concat_axis=0, tiled=True).reshape(
        slot_count, q_width + kv_width
    )
    pre_part, recv = lax.optimization_barrier((pre_part, recv))
    pre_out = lax.psum_scatter(pre_part, "tp", scatter_dimension=0, tiled=True)
    q_slots = recv[:, :q_width].reshape(slot_count, kv_heads, QPK, HD)
    kv_slots = recv[:, q_width:].reshape(slot_count, kv_heads, 2, HD)
    slot_attn = decode_block(q_slots, kv_slots, dec_table, pool_keys, pool_vals)
    replies = lax.all_to_all(
        slot_attn.reshape(groups, capacity, q_width), "req", split_axis=0, concat_axis=0, tiled=True
    )
    pre_out, replies = lax.optimization_barrier((pre_out, replies))
    dec_attn = lax.dot_general(
        dispatch,
        replies.reshape(slot_count, q_width),
        (((0,), (0,)), ((), ())),
        preferred_element_type=jnp.float32,
    ).astype(jnp.bfloat16)
    dec_out = lax.psum_scatter(
        term_maker(dec_attn, wo).astype(jnp.bfloat16), "tp", scatter_dimension=0, tiled=True
    )
    return (dec_out, pre_out)


def solution(mesh):
    placed = (
        P("req", "tp"),
        P("req", "tp"),
        P("req"),
        P("req", None),
        P("req", "tp"),
        P("req", "tp"),
        P("req", None),
        P("req", "tp"),
        P("tp", None),
    )
    return jax.shard_map(
        per_device,
        mesh=mesh,
        in_specs=placed,
        out_specs=(P(("req", "tp"), None), P(("req", "tp"), None)),
        check_vma=False,
    )
```

```python
import math

import jax
import jax.numpy as jnp
from jax import lax
from jax.sharding import PartitionSpec as P

HD = 128
QPK = 3


MASKED_SCORE = -1e30


def decode_block(q_block, kv_block, windows, pool_keys, pool_vals):
    score_scale = 1.0 / math.sqrt(HD)
    slot_rows = q_block.shape[0]
    places = lax.iota(jnp.int32, pool_keys.shape[0])
    begins = windows[:, 0:1]
    visible = (places[None, :] >= begins) & (places[None, :] < begins + windows[:, 1:2])
    visible = visible[:, None, None, :]
    pool_scores = (
        jnp.einsum("sghd,pgd->sghp", q_block, pool_keys, preferred_element_type=jnp.float32)
        * score_scale
    )
    pool_scores = jnp.where(visible, pool_scores, MASKED_SCORE)
    self_scores = (
        jnp.einsum(
            "sghd,sgd->sgh", q_block, kv_block[:, :, 0, :], preferred_element_type=jnp.float32
        )
        * score_scale
    )
    row_peak = jnp.maximum(jnp.max(pool_scores, axis=-1), self_scores)
    pool_exp = jnp.where(visible, jnp.exp(pool_scores - row_peak[..., None]), 0.0)
    self_exp = jnp.exp(self_scores - row_peak)
    row_total = jnp.sum(pool_exp, axis=-1) + self_exp
    pool_weight = (pool_exp / row_total[..., None]).astype(jnp.bfloat16)
    self_weight = (self_exp / row_total).astype(jnp.bfloat16)
    mixed_rows = jnp.einsum(
        "sghp,pgd->sghd", pool_weight, pool_vals, preferred_element_type=jnp.float32
    )
    mixed_rows = mixed_rows + self_weight.astype(jnp.float32)[..., None] * kv_block[
        :, :, None, 1, :
    ].astype(jnp.float32)
    return mixed_rows.astype(jnp.bfloat16).reshape(slot_rows, -1)


def prefill_attend(q_rows, kv_rows, meta_row, pool_keys, pool_vals, kv_heads):
    score_scale = 1.0 / math.sqrt(HD)
    span_rows = q_rows.shape[0]
    queries = q_rows.reshape(span_rows, kv_heads, QPK, HD)
    span_kv = kv_rows.reshape(span_rows, kv_heads, 2, HD)
    places = lax.iota(jnp.int32, pool_keys.shape[0])
    visible = (places >= meta_row[0]) & (places < meta_row[0] + meta_row[1])
    visible = visible[None, None, None, :]
    row_iota = lax.iota(jnp.int32, span_rows)
    causal = (row_iota[None, :] <= row_iota[:, None])[:, None, None, :]
    pool_scores = (
        jnp.einsum("jghd,pgd->jghp", queries, pool_keys, preferred_element_type=jnp.float32)
        * score_scale
    )
    pool_scores = jnp.where(visible, pool_scores, MASKED_SCORE)
    span_scores = (
        jnp.einsum(
            "jghd,igd->jghi", queries, span_kv[:, :, 0, :], preferred_element_type=jnp.float32
        )
        * score_scale
    )
    span_scores = jnp.where(causal, span_scores, MASKED_SCORE)
    row_peak = jnp.maximum(jnp.max(pool_scores, axis=-1), jnp.max(span_scores, axis=-1))
    pool_exp = jnp.where(visible, jnp.exp(pool_scores - row_peak[..., None]), 0.0)
    span_exp = jnp.where(causal, jnp.exp(span_scores - row_peak[..., None]), 0.0)
    row_total = jnp.sum(pool_exp, axis=-1) + jnp.sum(span_exp, axis=-1)
    pool_weight = (pool_exp / row_total[..., None]).astype(jnp.bfloat16)
    span_weight = (span_exp / row_total[..., None]).astype(jnp.bfloat16)
    mixed_rows = jnp.einsum(
        "jghp,pgd->jghd", pool_weight, pool_vals, preferred_element_type=jnp.float32
    )
    mixed_rows = mixed_rows + jnp.einsum(
        "jghi,igd->jghd", span_weight, span_kv[:, :, 1, :], preferred_element_type=jnp.float32
    )
    live = (row_iota < meta_row[2])[:, None, None, None]
    return jnp.where(live, mixed_rows, 0.0).astype(jnp.bfloat16).reshape(span_rows, -1)


def term_maker(rows_source, wo):
    return jnp.dot(rows_source, wo, preferred_element_type=jnp.float32)


def ring_sum_scatter(part, axis):
    n = lax.axis_size(axis)
    me = lax.axis_index(axis)
    rows = part.shape[0] // n
    half = rows // 2
    chunks = part.reshape(n, rows, part.shape[1])
    fwd_chunks = chunks[:, :half]
    bwd_chunks = chunks[:, half:]
    fwd_perm = [(i, (i + 1) % n) for i in range(n)]
    bwd_perm = [(i, (i + n - 1) % n) for i in range(n)]

    def pick(source, index):
        return lax.dynamic_index_in_dim(source, index % n, 0, keepdims=False).astype(jnp.float32)

    fwd = pick(fwd_chunks, me + n - 1)
    bwd = pick(bwd_chunks, me + 1)
    for step in range(n - 1):
        fwd = lax.ppermute(fwd, axis, fwd_perm) + pick(fwd_chunks, me + 2 * n - step - 2)
        bwd = lax.ppermute(bwd, axis, bwd_perm) + pick(bwd_chunks, me + step + 2)
    return jnp.concatenate([fwd, bwd], axis=0).astype(jnp.bfloat16)


def per_device(dec_q, dec_kv, dec_owner, dec_table, pre_q, pre_kv, pre_meta, pool, wo):
    groups = lax.axis_size("req")
    tok_rows = dec_q.shape[0]
    capacity = max(2, (2 * tok_rows + groups - 1) // groups)
    slot_count = groups * capacity
    q_width = dec_q.shape[1]
    kv_width = dec_kv.shape[1]
    kv_heads = pool.shape[1] // (2 * HD)
    pool_rows = pool.reshape(pool.shape[0], kv_heads, 2, HD)
    pool_keys = pool_rows[:, :, 0, :]
    pool_vals = pool_rows[:, :, 1, :]

    pre_attn = prefill_attend(pre_q, pre_kv, pre_meta[0], pool_keys, pool_vals, kv_heads)
    pre_part = term_maker(pre_attn, wo).astype(jnp.bfloat16)

    group_iota = lax.iota(jnp.int32, groups)
    hot_table = (dec_owner[:, None] == group_iota[None, :]).astype(jnp.int32)
    ranking = jnp.sum((jnp.cumsum(hot_table, axis=0) - hot_table) * hot_table, axis=1)
    slot_ids = dec_owner * capacity + ranking
    dispatch = (slot_ids[None, :] == lax.iota(jnp.int32, slot_count)[:, None]).astype(jnp.bfloat16)
    send = (
        jnp.dot(dispatch, jnp.concatenate([dec_q, dec_kv], axis=1), preferred_element_type=jnp.float32)
        .astype(jnp.bfloat16)
        .reshape(groups, capacity, q_width + kv_width)
    )
    recv = lax.all_to_all(send, "req", split_axis=0, concat_axis=0, tiled=True).reshape(
        slot_count, q_width + kv_width
    )
    pre_part, recv = lax.optimization_barrier((pre_part, recv))
    pre_out = lax.psum_scatter(pre_part, "tp", scatter_dimension=0, tiled=True)
    q_slots = recv[:, :q_width].reshape(slot_count, kv_heads, QPK, HD)
    kv_slots = recv[:, q_width:].reshape(slot_count, kv_heads, 2, HD)
    slot_attn = decode_block(q_slots, kv_slots, dec_table, pool_keys, pool_vals)
    replies = lax.all_to_all(
        slot_attn.reshape(groups, capacity, q_width), "req", split_axis=0, concat_axis=0, tiled=True
    )
    dec_attn = lax.dot_general(
        dispatch,
        replies.reshape(slot_count, q_width),
        (((0,), (0,)), ((), ())),
        preferred_element_type=jnp.float32,
    ).astype(jnp.bfloat16)
    dec_out = ring_sum_scatter(term_maker(dec_attn, wo).astype(jnp.bfloat16), "tp")
    return (dec_out, pre_out)


def solution(mesh):
    placed = (
        P("req", "tp"),
        P("req", "tp"),
        P("req"),
        P("req", None),
        P("req", "tp"),
        P("req", "tp"),
        P("req", None),
        P("req", "tp"),
        P("tp", None),
    )
    return jax.shard_map(
        per_device,
        mesh=mesh,
        in_specs=placed,
        out_specs=(P(("req", "tp"), None), P(("req", "tp"), None)),
        check_vma=False,
    )
```

```python
import math

import jax
import jax.numpy as jnp
from jax import lax
from jax.sharding import PartitionSpec as P

HD = 128
QPK = 3


MASKED_SCORE = -1e30


def decode_block(q_block, kv_block, windows, pool_keys, pool_vals):
    score_scale = 1.0 / math.sqrt(HD)
    slot_rows = q_block.shape[0]
    places = lax.iota(jnp.int32, pool_keys.shape[0])
    begins = windows[:, 0:1]
    visible = (places[None, :] >= begins) & (places[None, :] < begins + windows[:, 1:2])
    visible = visible[:, None, None, :]
    pool_scores = (
        jnp.einsum("sghd,pgd->sghp", q_block, pool_keys, preferred_element_type=jnp.float32)
        * score_scale
    )
    pool_scores = jnp.where(visible, pool_scores, MASKED_SCORE)
    self_scores = (
        jnp.einsum(
            "sghd,sgd->sgh", q_block, kv_block[:, :, 0, :], preferred_element_type=jnp.float32
        )
        * score_scale
    )
    row_peak = jnp.maximum(jnp.max(pool_scores, axis=-1), self_scores)
    pool_exp = jnp.where(visible, jnp.exp(pool_scores - row_peak[..., None]), 0.0)
    self_exp = jnp.exp(self_scores - row_peak)
    row_total = jnp.sum(pool_exp, axis=-1) + self_exp
    pool_weight = (pool_exp / row_total[..., None]).astype(jnp.bfloat16)
    self_weight = (self_exp / row_total).astype(jnp.bfloat16)
    mixed_rows = jnp.einsum(
        "sghp,pgd->sghd", pool_weight, pool_vals, preferred_element_type=jnp.float32
    )
    mixed_rows = mixed_rows + self_weight.astype(jnp.float32)[..., None] * kv_block[
        :, :, None, 1, :
    ].astype(jnp.float32)
    return mixed_rows.astype(jnp.bfloat16).reshape(slot_rows, -1)


def prefill_attend(q_rows, kv_rows, meta_row, pool_keys, pool_vals, kv_heads):
    score_scale = 1.0 / math.sqrt(HD)
    span_rows = q_rows.shape[0]
    queries = q_rows.reshape(span_rows, kv_heads, QPK, HD)
    span_kv = kv_rows.reshape(span_rows, kv_heads, 2, HD)
    places = lax.iota(jnp.int32, pool_keys.shape[0])
    visible = (places >= meta_row[0]) & (places < meta_row[0] + meta_row[1])
    visible = visible[None, None, None, :]
    row_iota = lax.iota(jnp.int32, span_rows)
    causal = (row_iota[None, :] <= row_iota[:, None])[:, None, None, :]
    pool_scores = (
        jnp.einsum("jghd,pgd->jghp", queries, pool_keys, preferred_element_type=jnp.float32)
        * score_scale
    )
    pool_scores = jnp.where(visible, pool_scores, MASKED_SCORE)
    span_scores = (
        jnp.einsum(
            "jghd,igd->jghi", queries, span_kv[:, :, 0, :], preferred_element_type=jnp.float32
        )
        * score_scale
    )
    span_scores = jnp.where(causal, span_scores, MASKED_SCORE)
    row_peak = jnp.maximum(jnp.max(pool_scores, axis=-1), jnp.max(span_scores, axis=-1))
    pool_exp = jnp.where(visible, jnp.exp(pool_scores - row_peak[..., None]), 0.0)
    span_exp = jnp.where(causal, jnp.exp(span_scores - row_peak[..., None]), 0.0)
    row_total = jnp.sum(pool_exp, axis=-1) + jnp.sum(span_exp, axis=-1)
    pool_weight = (pool_exp / row_total[..., None]).astype(jnp.bfloat16)
    span_weight = (span_exp / row_total[..., None]).astype(jnp.bfloat16)
    mixed_rows = jnp.einsum(
        "jghp,pgd->jghd", pool_weight, pool_vals, preferred_element_type=jnp.float32
    )
    mixed_rows = mixed_rows + jnp.einsum(
        "jghi,igd->jghd", span_weight, span_kv[:, :, 1, :], preferred_element_type=jnp.float32
    )
    live = (row_iota < meta_row[2])[:, None, None, None]
    return jnp.where(live, mixed_rows, 0.0).astype(jnp.bfloat16).reshape(span_rows, -1)


def term_maker(rows_source, wo):
    return jnp.dot(rows_source, wo, preferred_element_type=jnp.float32)


def per_device(dec_q, dec_kv, dec_owner, dec_table, pre_q, pre_kv, pre_meta, pool, wo):
    groups = lax.axis_size("req")
    tok_rows = dec_q.shape[0]
    capacity = max(2, (2 * tok_rows + groups - 1) // groups)
    slot_count = groups * capacity
    q_width = dec_q.shape[1]
    kv_width = dec_kv.shape[1]
    kv_heads = pool.shape[1] // (2 * HD)
    pool_rows = pool.reshape(pool.shape[0], kv_heads, 2, HD)
    pool_keys = pool_rows[:, :, 0, :]
    pool_vals = pool_rows[:, :, 1, :]

    pre_attn = prefill_attend(pre_q, pre_kv, pre_meta[0], pool_keys, pool_vals, kv_heads)
    pre_part = term_maker(pre_attn, wo).astype(jnp.bfloat16)

    group_iota = lax.iota(jnp.int32, groups)
    hot_table = (dec_owner[:, None] == group_iota[None, :]).astype(jnp.int32)
    ranking = jnp.sum((jnp.cumsum(hot_table, axis=0) - hot_table) * hot_table, axis=1)
    slot_ids = dec_owner * capacity + ranking
    dispatch = (slot_ids[None, :] == lax.iota(jnp.int32, slot_count)[:, None]).astype(jnp.bfloat16)
    send = (
        jnp.dot(dispatch, jnp.concatenate([dec_q, dec_kv], axis=1), preferred_element_type=jnp.float32)
        .astype(jnp.bfloat16)
        .reshape(groups, capacity, q_width + kv_width)
    )
    recv = lax.all_to_all(send, "req", split_axis=0, concat_axis=0, tiled=True).reshape(
        slot_count, q_width + kv_width
    )
    pre_part, recv = lax.optimization_barrier((pre_part, recv))
    pre_out = lax.psum_scatter(pre_part, "tp", scatter_dimension=0, tiled=True)
    q_slots = recv[:, :q_width].reshape(slot_count, kv_heads, QPK, HD)
    kv_slots = recv[:, q_width:].reshape(slot_count, kv_heads, 2, HD)
    slot_attn = decode_block(q_slots, kv_slots, dec_table, pool_keys, pool_vals)
    replies = lax.all_to_all(
        slot_attn.reshape(groups, capacity, q_width), "req", split_axis=0, concat_axis=0, tiled=True
    )
    dec_attn = lax.dot_general(
        dispatch,
        replies.reshape(slot_count, q_width),
        (((0,), (0,)), ((), ())),
        preferred_element_type=jnp.float32,
    ).astype(jnp.bfloat16)
    tp_count = lax.axis_size("tp")
    dec_part = term_maker(dec_attn, wo).astype(jnp.bfloat16)
    pieces = lax.all_to_all(
        dec_part.reshape(tp_count, tok_rows // tp_count, dec_part.shape[1]),
        "tp",
        split_axis=0,
        concat_axis=0,
        tiled=True,
    )
    dec_out = jnp.sum(pieces.astype(jnp.float32), axis=0).astype(jnp.bfloat16)
    return (dec_out, pre_out)


def solution(mesh):
    placed = (
        P("req", "tp"),
        P("req", "tp"),
        P("req"),
        P("req", None),
        P("req", "tp"),
        P("req", "tp"),
        P("req", None),
        P("req", "tp"),
        P("tp", None),
    )
    return jax.shard_map(
        per_device,
        mesh=mesh,
        in_specs=placed,
        out_specs=(P(("req", "tp"), None), P(("req", "tp"), None)),
        check_vma=False,
    )
```

```python
import math

import jax
import jax.numpy as jnp
from jax import lax
from jax.sharding import PartitionSpec as P

HD = 128
QPK = 3


MASKED_SCORE = -1e30


def decode_block(q_block, kv_block, windows, pool_keys, pool_vals):
    score_scale = 1.0 / math.sqrt(HD)
    slot_rows = q_block.shape[0]
    places = lax.iota(jnp.int32, pool_keys.shape[0])
    begins = windows[:, 0:1]
    visible = (places[None, :] >= begins) & (places[None, :] < begins + windows[:, 1:2])
    visible = visible[:, None, None, :]
    pool_scores = (
        jnp.einsum("sghd,pgd->sghp", q_block, pool_keys, preferred_element_type=jnp.float32)
        * score_scale
    )
    pool_scores = jnp.where(visible, pool_scores, MASKED_SCORE)
    self_scores = (
        jnp.einsum(
            "sghd,sgd->sgh", q_block, kv_block[:, :, 0, :], preferred_element_type=jnp.float32
        )
        * score_scale
    )
    row_peak = jnp.maximum(jnp.max(pool_scores, axis=-1), self_scores)
    pool_exp = jnp.where(visible, jnp.exp(pool_scores - row_peak[..., None]), 0.0)
    self_exp = jnp.exp(self_scores - row_peak)
    row_total = jnp.sum(pool_exp, axis=-1) + self_exp
    pool_weight = (pool_exp / row_total[..., None]).astype(jnp.bfloat16)
    self_weight = (self_exp / row_total).astype(jnp.bfloat16)
    mixed_rows = jnp.einsum(
        "sghp,pgd->sghd", pool_weight, pool_vals, preferred_element_type=jnp.float32
    )
    mixed_rows = mixed_rows + self_weight.astype(jnp.float32)[..., None] * kv_block[
        :, :, None, 1, :
    ].astype(jnp.float32)
    return mixed_rows.astype(jnp.bfloat16).reshape(slot_rows, -1)


def prefill_attend(q_rows, kv_rows, meta_row, pool_keys, pool_vals, kv_heads):
    score_scale = 1.0 / math.sqrt(HD)
    span_rows = q_rows.shape[0]
    queries = q_rows.reshape(span_rows, kv_heads, QPK, HD)
    span_kv = kv_rows.reshape(span_rows, kv_heads, 2, HD)
    places = lax.iota(jnp.int32, pool_keys.shape[0])
    visible = (places >= meta_row[0]) & (places < meta_row[0] + meta_row[1])
    visible = visible[None, None, None, :]
    row_iota = lax.iota(jnp.int32, span_rows)
    causal = (row_iota[None, :] <= row_iota[:, None])[:, None, None, :]
    pool_scores = (
        jnp.einsum("jghd,pgd->jghp", queries, pool_keys, preferred_element_type=jnp.float32)
        * score_scale
    )
    pool_scores = jnp.where(visible, pool_scores, MASKED_SCORE)
    span_scores = (
        jnp.einsum(
            "jghd,igd->jghi", queries, span_kv[:, :, 0, :], preferred_element_type=jnp.float32
        )
        * score_scale
    )
    span_scores = jnp.where(causal, span_scores, MASKED_SCORE)
    row_peak = jnp.maximum(jnp.max(pool_scores, axis=-1), jnp.max(span_scores, axis=-1))
    pool_exp = jnp.where(visible, jnp.exp(pool_scores - row_peak[..., None]), 0.0)
    span_exp = jnp.where(causal, jnp.exp(span_scores - row_peak[..., None]), 0.0)
    row_total = jnp.sum(pool_exp, axis=-1) + jnp.sum(span_exp, axis=-1)
    pool_weight = (pool_exp / row_total[..., None]).astype(jnp.bfloat16)
    span_weight = (span_exp / row_total[..., None]).astype(jnp.bfloat16)
    mixed_rows = jnp.einsum(
        "jghp,pgd->jghd", pool_weight, pool_vals, preferred_element_type=jnp.float32
    )
    mixed_rows = mixed_rows + jnp.einsum(
        "jghi,igd->jghd", span_weight, span_kv[:, :, 1, :], preferred_element_type=jnp.float32
    )
    live = (row_iota < meta_row[2])[:, None, None, None]
    return jnp.where(live, mixed_rows, 0.0).astype(jnp.bfloat16).reshape(span_rows, -1)


def term_maker(rows_source, wo):
    return jnp.dot(rows_source, wo, preferred_element_type=jnp.float32)


def per_device(dec_q, dec_kv, dec_owner, dec_table, pre_q, pre_kv, pre_meta, pool, wo):
    groups = lax.axis_size("req")
    tok_rows = dec_q.shape[0]
    capacity = max(2, (2 * tok_rows + groups - 1) // groups)
    slot_count = groups * capacity
    q_width = dec_q.shape[1]
    kv_width = dec_kv.shape[1]
    kv_heads = pool.shape[1] // (2 * HD)
    pool_rows = pool.reshape(pool.shape[0], kv_heads, 2, HD)
    pool_keys = pool_rows[:, :, 0, :]
    pool_vals = pool_rows[:, :, 1, :]

    pre_attn = prefill_attend(pre_q, pre_kv, pre_meta[0], pool_keys, pool_vals, kv_heads)
    pre_part = term_maker(pre_attn, wo).astype(jnp.bfloat16)

    tok_iota = lax.iota(jnp.int32, tok_rows)
    earlier_same = (dec_owner[:, None] == dec_owner[None, :]) & (tok_iota[None, :] < tok_iota[:, None])
    ranking = jnp.sum(earlier_same.astype(jnp.int32), axis=1)
    slot_ids = dec_owner * capacity + ranking
    dispatch = (slot_ids[None, :] == lax.iota(jnp.int32, slot_count)[:, None]).astype(jnp.bfloat16)
    send = (
        jnp.dot(dispatch, jnp.concatenate([dec_q, dec_kv], axis=1), preferred_element_type=jnp.float32)
        .astype(jnp.bfloat16)
        .reshape(groups, capacity, q_width + kv_width)
    )
    recv = lax.all_to_all(send, "req", split_axis=0, concat_axis=0, tiled=True).reshape(
        slot_count, q_width + kv_width
    )
    pre_part, recv = lax.optimization_barrier((pre_part, recv))
    pre_out = lax.psum_scatter(pre_part, "tp", scatter_dimension=0, tiled=True)
    q_slots = recv[:, :q_width].reshape(slot_count, kv_heads, QPK, HD)
    kv_slots = recv[:, q_width:].reshape(slot_count, kv_heads, 2, HD)
    slot_attn = decode_block(q_slots, kv_slots, dec_table, pool_keys, pool_vals)
    replies = lax.all_to_all(
        slot_attn.reshape(groups, capacity, q_width), "req", split_axis=0, concat_axis=0, tiled=True
    )
    dec_attn = lax.dot_general(
        dispatch,
        replies.reshape(slot_count, q_width),
        (((0,), (0,)), ((), ())),
        preferred_element_type=jnp.float32,
    ).astype(jnp.bfloat16)
    tp_count = lax.axis_size("tp")
    dec_part = term_maker(dec_attn, wo).astype(jnp.bfloat16)
    pieces = lax.all_to_all(
        dec_part.reshape(tp_count, tok_rows // tp_count, dec_part.shape[1]),
        "tp",
        split_axis=0,
        concat_axis=0,
        tiled=True,
    )
    dec_out = jnp.sum(pieces.astype(jnp.float32), axis=0).astype(jnp.bfloat16)
    return (dec_out, pre_out)


def solution(mesh):
    placed = (
        P("req", "tp"),
        P("req", "tp"),
        P("req"),
        P("req", None),
        P("req", "tp"),
        P("req", "tp"),
        P("req", None),
        P("req", "tp"),
        P("tp", None),
    )
    return jax.shard_map(
        per_device,
        mesh=mesh,
        in_specs=placed,
        out_specs=(P(("req", "tp"), None), P(("req", "tp"), None)),
        check_vma=False,
    )
```

```python
import math

import jax
import jax.numpy as jnp
from jax import lax
from jax.experimental import pallas as pl
from jax.experimental.pallas import tpu as pltpu
from jax.sharding import PartitionSpec as P

HD = 128
QPK = 3


MASKED_SCORE = -1e30


def decode_kernel(recv_ref, table_ref, pool_ref, out_ref):
    score_scale = 1.0 / math.sqrt(HD)
    slot_rows = recv_ref.shape[0]
    kv_heads = pool_ref.shape[1] // (2 * HD)
    q_width = kv_heads * QPK * HD
    table = table_ref[...]
    begins = table[:, 0:1]
    ends = begins + table[:, 1:2]
    places = lax.broadcasted_iota(jnp.int32, (slot_rows, pool_ref.shape[0]), 1)
    visible = (places >= begins) & (places < ends)
    for g in range(kv_heads):
        keys = pool_ref[:, g * 2 * HD : g * 2 * HD + HD]
        vals = pool_ref[:, g * 2 * HD + HD : (g + 1) * 2 * HD]
        own_key = recv_ref[:, q_width + g * 2 * HD : q_width + g * 2 * HD + HD].astype(jnp.float32)
        own_val = recv_ref[:, q_width + g * 2 * HD + HD : q_width + (g + 1) * 2 * HD].astype(jnp.float32)
        for h in range(QPK):
            col = (g * QPK + h) * HD
            q = recv_ref[:, col : col + HD]
            scores = lax.dot_general(
                q, keys, (((1,), (1,)), ((), ())), preferred_element_type=jnp.float32
            ) * score_scale
            scores = jnp.where(visible, scores, MASKED_SCORE)
            own = jnp.sum(q.astype(jnp.float32) * own_key, axis=1, keepdims=True) * score_scale
            peak = jnp.maximum(jnp.max(scores, axis=1, keepdims=True), own)
            weights = jnp.where(visible, jnp.exp(scores - peak), 0.0)
            own_exp = jnp.exp(own - peak)
            total = jnp.sum(weights, axis=1, keepdims=True) + own_exp
            weights = (weights / total).astype(jnp.bfloat16)
            own_weight = (own_exp / total).astype(jnp.bfloat16).astype(jnp.float32)
            mixed = jnp.dot(weights, vals, preferred_element_type=jnp.float32) + own_weight * own_val
            out_ref[:, col : col + HD] = mixed.astype(jnp.bfloat16)


def prefill_kernel(q_ref, kv_ref, meta_ref, pool_ref, out_ref):
    score_scale = 1.0 / math.sqrt(HD)
    span_rows = q_ref.shape[0]
    pool_len = pool_ref.shape[0]
    kv_heads = pool_ref.shape[1] // (2 * HD)
    meta = meta_ref[...]
    begin = meta[:, 0:1]
    end = begin + meta[:, 1:2]
    places = lax.broadcasted_iota(jnp.int32, (span_rows, pool_len), 1)
    visible = (places >= begin) & (places < end)
    row_iota = lax.broadcasted_iota(jnp.int32, (span_rows, span_rows), 0)
    col_iota = lax.broadcasted_iota(jnp.int32, (span_rows, span_rows), 1)
    causal = col_iota <= row_iota
    live = lax.broadcasted_iota(jnp.int32, (span_rows, 1), 0) < meta[:, 2:3]
    for g in range(kv_heads):
        keys = pool_ref[:, g * 2 * HD : g * 2 * HD + HD]
        vals = pool_ref[:, g * 2 * HD + HD : (g + 1) * 2 * HD]
        span_keys = kv_ref[:, g * 2 * HD : g * 2 * HD + HD]
        span_vals = kv_ref[:, g * 2 * HD + HD : (g + 1) * 2 * HD]
        for h in range(QPK):
            col = (g * QPK + h) * HD
            q = q_ref[:, col : col + HD]
            dims = (((1,), (1,)), ((), ()))
            pool_scores = lax.dot_general(q, keys, dims, preferred_element_type=jnp.float32) * score_scale
            pool_scores = jnp.where(visible, pool_scores, MASKED_SCORE)
            span_scores = lax.dot_general(q, span_keys, dims, preferred_element_type=jnp.float32) * score_scale
            span_scores = jnp.where(causal, span_scores, MASKED_SCORE)
            peak = jnp.maximum(
                jnp.max(pool_scores, axis=1, keepdims=True), jnp.max(span_scores, axis=1, keepdims=True)
            )
            pool_exp = jnp.where(visible, jnp.exp(pool_scores - peak), 0.0)
            span_exp = jnp.where(causal, jnp.exp(span_scores - peak), 0.0)
            total = jnp.sum(pool_exp, axis=1, keepdims=True) + jnp.sum(span_exp, axis=1, keepdims=True)
            pool_weight = (pool_exp / total).astype(jnp.bfloat16)
            span_weight = (span_exp / total).astype(jnp.bfloat16)
            mixed = jnp.dot(pool_weight, vals, preferred_element_type=jnp.float32) + jnp.dot(
                span_weight, span_vals, preferred_element_type=jnp.float32
            )
            out_ref[:, col : col + HD] = jnp.where(live, mixed, 0.0).astype(jnp.bfloat16)


def vmem_call(kernel, out_shape, operands, flops, transcendentals):
    bytes_accessed = sum(x.size * x.dtype.itemsize for x in operands) + out_shape.size * 2
    return pl.pallas_call(
        kernel,
        out_shape=out_shape,
        in_specs=[pl.BlockSpec(memory_space=pltpu.VMEM)] * len(operands),
        out_specs=pl.BlockSpec(memory_space=pltpu.VMEM),
        cost_estimate=pl.CostEstimate(
            flops=flops, transcendentals=transcendentals, bytes_accessed=bytes_accessed
        ),
    )(*operands)


def term_maker(rows_source, wo):
    return jnp.dot(rows_source, wo, preferred_element_type=jnp.float32)


def per_device(dec_q, dec_kv, dec_owner, dec_table, pre_q, pre_kv, pre_meta, pool, wo):
    groups = lax.axis_size("req")
    tok_rows = dec_q.shape[0]
    capacity = max(2, (2 * tok_rows + groups - 1) // groups)
    slot_count = groups * capacity
    q_width = dec_q.shape[1]
    kv_width = dec_kv.shape[1]

    span_rows = pre_q.shape[0]
    pre_attn = vmem_call(
        prefill_kernel,
        jax.ShapeDtypeStruct((span_rows, q_width), jnp.bfloat16),
        (pre_q, pre_kv, pre_meta, pool),
        4 * span_rows * (pool.shape[0] + span_rows) * q_width,
        span_rows * (pool.shape[0] + span_rows) * q_width // HD,
    )
    pre_part = term_maker(pre_attn, wo).astype(jnp.bfloat16)

    tok_iota = lax.iota(jnp.int32, tok_rows)
    earlier_same = (dec_owner[:, None] == dec_owner[None, :]) & (tok_iota[None, :] < tok_iota[:, None])
    ranking = jnp.sum(earlier_same.astype(jnp.int32), axis=1)
    slot_ids = dec_owner * capacity + ranking
    dispatch = (slot_ids[None, :] == lax.iota(jnp.int32, slot_count)[:, None]).astype(jnp.bfloat16)
    send = (
        jnp.dot(dispatch, jnp.concatenate([dec_q, dec_kv], axis=1), preferred_element_type=jnp.float32)
        .astype(jnp.bfloat16)
        .reshape(groups, capacity, q_width + kv_width)
    )
    recv = lax.all_to_all(send, "req", split_axis=0, concat_axis=0, tiled=True).reshape(
        slot_count, q_width + kv_width
    )
    pre_part, recv = lax.optimization_barrier((pre_part, recv))
    pre_out = lax.psum_scatter(pre_part, "tp", scatter_dimension=0, tiled=True)
    slot_attn = vmem_call(
        decode_kernel,
        jax.ShapeDtypeStruct((slot_count, q_width), jnp.bfloat16),
        (recv, dec_table, pool),
        4 * slot_count * pool.shape[0] * q_width,
        slot_count * pool.shape[0] * q_width // HD,
    )
    replies = lax.all_to_all(
        slot_attn.reshape(groups, capacity, q_width), "req", split_axis=0, concat_axis=0, tiled=True
    )
    dec_attn = lax.dot_general(
        dispatch,
        replies.reshape(slot_count, q_width),
        (((0,), (0,)), ((), ())),
        preferred_element_type=jnp.float32,
    ).astype(jnp.bfloat16)
    tp_count = lax.axis_size("tp")
    dec_part = term_maker(dec_attn, wo).astype(jnp.bfloat16)
    pieces = lax.all_to_all(
        dec_part.reshape(tp_count, tok_rows // tp_count, dec_part.shape[1]),
        "tp",
        split_axis=0,
        concat_axis=0,
        tiled=True,
    )
    dec_out = jnp.sum(pieces.astype(jnp.float32), axis=0).astype(jnp.bfloat16)
    return (dec_out, pre_out)


def solution(mesh):
    placed = (
        P("req", "tp"),
        P("req", "tp"),
        P("req"),
        P("req", None),
        P("req", "tp"),
        P("req", "tp"),
        P("req", None),
        P("req", "tp"),
        P("tp", None),
    )
    return jax.shard_map(
        per_device,
        mesh=mesh,
        in_specs=placed,
        out_specs=(P(("req", "tp"), None), P(("req", "tp"), None)),
        check_vma=False,
    )
```

```python
import math

import jax
import jax.numpy as jnp
from jax import lax
from jax.experimental import pallas as pl
from jax.experimental.pallas import tpu as pltpu
from jax.sharding import PartitionSpec as P

HD = 128
QPK = 3


MASKED_SCORE = -1e30


def decode_kernel(recv_ref, table_ref, pool_ref, out_ref):
    score_scale = 1.0 / math.sqrt(HD)
    slot_rows = recv_ref.shape[0]
    kv_heads = pool_ref.shape[1] // (2 * HD)
    q_width = kv_heads * QPK * HD
    table = table_ref[...]
    begins = table[:, 0:1]
    ends = begins + table[:, 1:2]
    places = lax.broadcasted_iota(jnp.int32, (slot_rows, pool_ref.shape[0]), 1)
    visible = (places >= begins) & (places < ends)
    for g in range(kv_heads):
        keys = pool_ref[:, g * 2 * HD : g * 2 * HD + HD]
        vals = pool_ref[:, g * 2 * HD + HD : (g + 1) * 2 * HD]
        own_key = recv_ref[:, q_width + g * 2 * HD : q_width + g * 2 * HD + HD].astype(jnp.float32)
        own_val = recv_ref[:, q_width + g * 2 * HD + HD : q_width + (g + 1) * 2 * HD].astype(jnp.float32)
        for h in range(QPK):
            col = (g * QPK + h) * HD
            q = recv_ref[:, col : col + HD]
            scores = lax.dot_general(
                q, keys, (((1,), (1,)), ((), ())), preferred_element_type=jnp.float32
            ) * score_scale
            scores = jnp.where(visible, scores, MASKED_SCORE)
            own = jnp.sum(q.astype(jnp.float32) * own_key, axis=1, keepdims=True) * score_scale
            peak = jnp.maximum(jnp.max(scores, axis=1, keepdims=True), own)
            weights = jnp.where(visible, jnp.exp(scores - peak), 0.0)
            own_exp = jnp.exp(own - peak)
            total = jnp.sum(weights, axis=1, keepdims=True) + own_exp
            weights = (weights / total).astype(jnp.bfloat16)
            own_weight = (own_exp / total).astype(jnp.bfloat16).astype(jnp.float32)
            mixed = jnp.dot(weights, vals, preferred_element_type=jnp.float32) + own_weight * own_val
            out_ref[:, col : col + HD] = mixed.astype(jnp.bfloat16)


def prefill_kernel(q_ref, kv_ref, meta_ref, pool_ref, out_ref):
    score_scale = 1.0 / math.sqrt(HD)
    span_rows = q_ref.shape[0]
    pool_len = pool_ref.shape[0]
    kv_heads = pool_ref.shape[1] // (2 * HD)
    meta = meta_ref[...]
    begin = meta[:, 0:1]
    end = begin + meta[:, 1:2]
    places = lax.broadcasted_iota(jnp.int32, (span_rows, pool_len), 1)
    visible = (places >= begin) & (places < end)
    row_iota = lax.broadcasted_iota(jnp.int32, (span_rows, span_rows), 0)
    col_iota = lax.broadcasted_iota(jnp.int32, (span_rows, span_rows), 1)
    causal = col_iota <= row_iota
    live = lax.broadcasted_iota(jnp.int32, (span_rows, 1), 0) < meta[:, 2:3]
    for g in range(kv_heads):
        keys = pool_ref[:, g * 2 * HD : g * 2 * HD + HD]
        vals = pool_ref[:, g * 2 * HD + HD : (g + 1) * 2 * HD]
        span_keys = kv_ref[:, g * 2 * HD : g * 2 * HD + HD]
        span_vals = kv_ref[:, g * 2 * HD + HD : (g + 1) * 2 * HD]
        for h in range(QPK):
            col = (g * QPK + h) * HD
            q = q_ref[:, col : col + HD]
            dims = (((1,), (1,)), ((), ()))
            pool_scores = lax.dot_general(q, keys, dims, preferred_element_type=jnp.float32) * score_scale
            pool_scores = jnp.where(visible, pool_scores, MASKED_SCORE)
            span_scores = lax.dot_general(q, span_keys, dims, preferred_element_type=jnp.float32) * score_scale
            span_scores = jnp.where(causal, span_scores, MASKED_SCORE)
            peak = jnp.maximum(
                jnp.max(pool_scores, axis=1, keepdims=True), jnp.max(span_scores, axis=1, keepdims=True)
            )
            pool_exp = jnp.where(visible, jnp.exp(pool_scores - peak), 0.0)
            span_exp = jnp.where(causal, jnp.exp(span_scores - peak), 0.0)
            total = jnp.sum(pool_exp, axis=1, keepdims=True) + jnp.sum(span_exp, axis=1, keepdims=True)
            pool_weight = (pool_exp / total).astype(jnp.bfloat16)
            span_weight = (span_exp / total).astype(jnp.bfloat16)
            mixed = jnp.dot(pool_weight, vals, preferred_element_type=jnp.float32) + jnp.dot(
                span_weight, span_vals, preferred_element_type=jnp.float32
            )
            out_ref[:, col : col + HD] = jnp.where(live, mixed, 0.0).astype(jnp.bfloat16)


def vmem_call(kernel, out_shape, operands, flops, transcendentals):
    bytes_accessed = sum(x.size * x.dtype.itemsize for x in operands) + out_shape.size * 2
    return pl.pallas_call(
        kernel,
        out_shape=out_shape,
        in_specs=[pl.BlockSpec(memory_space=pltpu.VMEM)] * len(operands),
        out_specs=pl.BlockSpec(memory_space=pltpu.VMEM),
        cost_estimate=pl.CostEstimate(
            flops=flops, transcendentals=transcendentals, bytes_accessed=bytes_accessed
        ),
    )(*operands)


def term_maker(rows_source, wo):
    return jnp.dot(rows_source, wo, preferred_element_type=jnp.float32)


def per_device(dec_q, dec_kv, dec_owner, dec_table, pre_q, pre_kv, pre_meta, pool, wo):
    groups = lax.axis_size("req")
    tok_rows = dec_q.shape[0]
    capacity = max(2, (2 * tok_rows + groups - 1) // groups)
    slot_count = groups * capacity
    q_width = dec_q.shape[1]
    kv_width = dec_kv.shape[1]

    span_rows = pre_q.shape[0]
    pre_attn = vmem_call(
        prefill_kernel,
        jax.ShapeDtypeStruct((span_rows, q_width), jnp.bfloat16),
        (pre_q, pre_kv, pre_meta, pool),
        4 * span_rows * (pool.shape[0] + span_rows) * q_width,
        span_rows * (pool.shape[0] + span_rows) * q_width // HD,
    )
    pre_part = term_maker(pre_attn, wo).astype(jnp.bfloat16)

    tok_iota = lax.iota(jnp.int32, tok_rows)
    earlier_same = (dec_owner[:, None] == dec_owner[None, :]) & (tok_iota[None, :] < tok_iota[:, None])
    ranking = jnp.sum(earlier_same.astype(jnp.int32), axis=1)
    slot_ids = dec_owner * capacity + ranking
    dispatch = (slot_ids[None, :] == lax.iota(jnp.int32, slot_count)[:, None]).astype(jnp.bfloat16)
    send = (
        jnp.dot(dispatch, jnp.concatenate([dec_q, dec_kv], axis=1), preferred_element_type=jnp.float32)
        .astype(jnp.bfloat16)
        .reshape(groups, capacity, q_width + kv_width)
    )
    pre_part, send = lax.optimization_barrier((pre_part, send))
    recv = lax.all_to_all(send, "req", split_axis=0, concat_axis=0, tiled=True).reshape(
        slot_count, q_width + kv_width
    )
    pre_out = lax.psum_scatter(pre_part, "tp", scatter_dimension=0, tiled=True)
    slot_attn = vmem_call(
        decode_kernel,
        jax.ShapeDtypeStruct((slot_count, q_width), jnp.bfloat16),
        (recv, dec_table, pool),
        4 * slot_count * pool.shape[0] * q_width,
        slot_count * pool.shape[0] * q_width // HD,
    )
    replies = lax.all_to_all(
        slot_attn.reshape(groups, capacity, q_width), "req", split_axis=0, concat_axis=0, tiled=True
    )
    dec_attn = lax.dot_general(
        dispatch,
        replies.reshape(slot_count, q_width),
        (((0,), (0,)), ((), ())),
        preferred_element_type=jnp.float32,
    ).astype(jnp.bfloat16)
    tp_count = lax.axis_size("tp")
    dec_part = term_maker(dec_attn, wo).astype(jnp.bfloat16)
    pieces = lax.all_to_all(
        dec_part.reshape(tp_count, tok_rows // tp_count, dec_part.shape[1]),
        "tp",
        split_axis=0,
        concat_axis=0,
        tiled=True,
    )
    dec_out = jnp.sum(pieces.astype(jnp.float32), axis=0).astype(jnp.bfloat16)
    return (dec_out, pre_out)


def solution(mesh):
    placed = (
        P("req", "tp"),
        P("req", "tp"),
        P("req"),
        P("req", None),
        P("req", "tp"),
        P("req", "tp"),
        P("req", None),
        P("req", "tp"),
        P("tp", None),
    )
    return jax.shard_map(
        per_device,
        mesh=mesh,
        in_specs=placed,
        out_specs=(P(("req", "tp"), None), P(("req", "tp"), None)),
        check_vma=False,
    )
```

```python
import math

import jax
import jax.numpy as jnp
from jax import lax
from jax.experimental import pallas as pl
from jax.experimental.pallas import tpu as pltpu
from jax.sharding import PartitionSpec as P

HD = 128
QPK = 3


MASKED_SCORE = -1e30


def decode_kernel(recv_ref, table_ref, pool_ref, out_ref):
    score_scale = 1.0 / math.sqrt(HD)
    slot_rows = recv_ref.shape[0]
    kv_heads = pool_ref.shape[1] // (2 * HD)
    q_width = kv_heads * QPK * HD
    table = table_ref[...]
    spread = jnp.broadcast_to(table[0:1, :], (HD, slot_rows))
    begins = jnp.transpose(spread)[:, 0:1]
    ends = begins + jnp.transpose(jnp.broadcast_to(table[1:2, :], (HD, slot_rows)))[:, 0:1]
    places = lax.broadcasted_iota(jnp.int32, (slot_rows, pool_ref.shape[0]), 1)
    visible = (places >= begins) & (places < ends)
    for g in range(kv_heads):
        keys = pool_ref[:, g * 2 * HD : g * 2 * HD + HD]
        vals = pool_ref[:, g * 2 * HD + HD : (g + 1) * 2 * HD]
        own_key = recv_ref[:, q_width + g * 2 * HD : q_width + g * 2 * HD + HD].astype(jnp.float32)
        own_val = recv_ref[:, q_width + g * 2 * HD + HD : q_width + (g + 1) * 2 * HD].astype(jnp.float32)
        for h in range(QPK):
            col = (g * QPK + h) * HD
            q = recv_ref[:, col : col + HD]
            scores = lax.dot_general(
                q, keys, (((1,), (1,)), ((), ())), preferred_element_type=jnp.float32
            ) * score_scale
            scores = jnp.where(visible, scores, MASKED_SCORE)
            own = jnp.sum(q.astype(jnp.float32) * own_key, axis=1, keepdims=True) * score_scale
            peak = jnp.maximum(jnp.max(scores, axis=1, keepdims=True), own)
            weights = jnp.where(visible, jnp.exp(scores - peak), 0.0)
            own_exp = jnp.exp(own - peak)
            total = jnp.sum(weights, axis=1, keepdims=True) + own_exp
            weights = (weights / total).astype(jnp.bfloat16)
            own_weight = (own_exp / total).astype(jnp.bfloat16).astype(jnp.float32)
            mixed = jnp.dot(weights, vals, preferred_element_type=jnp.float32) + own_weight * own_val
            out_ref[:, col : col + HD] = mixed.astype(jnp.bfloat16)


def prefill_kernel(q_ref, kv_ref, meta_ref, pool_ref, out_ref):
    score_scale = 1.0 / math.sqrt(HD)
    span_rows = q_ref.shape[0]
    pool_len = pool_ref.shape[0]
    kv_heads = pool_ref.shape[1] // (2 * HD)
    meta = meta_ref[...]
    begin = meta[:, 0:1]
    end = begin + meta[:, 1:2]
    places = lax.broadcasted_iota(jnp.int32, (span_rows, pool_len), 1)
    visible = (places >= begin) & (places < end)
    row_iota = lax.broadcasted_iota(jnp.int32, (span_rows, span_rows), 0)
    col_iota = lax.broadcasted_iota(jnp.int32, (span_rows, span_rows), 1)
    causal = col_iota <= row_iota
    live = lax.broadcasted_iota(jnp.int32, (span_rows, 1), 0) < meta[:, 2:3]
    for g in range(kv_heads):
        keys = pool_ref[:, g * 2 * HD : g * 2 * HD + HD]
        vals = pool_ref[:, g * 2 * HD + HD : (g + 1) * 2 * HD]
        span_keys = kv_ref[:, g * 2 * HD : g * 2 * HD + HD]
        span_vals = kv_ref[:, g * 2 * HD + HD : (g + 1) * 2 * HD]
        for h in range(QPK):
            col = (g * QPK + h) * HD
            q = q_ref[:, col : col + HD]
            dims = (((1,), (1,)), ((), ()))
            pool_scores = lax.dot_general(q, keys, dims, preferred_element_type=jnp.float32) * score_scale
            pool_scores = jnp.where(visible, pool_scores, MASKED_SCORE)
            span_scores = lax.dot_general(q, span_keys, dims, preferred_element_type=jnp.float32) * score_scale
            span_scores = jnp.where(causal, span_scores, MASKED_SCORE)
            peak = jnp.maximum(
                jnp.max(pool_scores, axis=1, keepdims=True), jnp.max(span_scores, axis=1, keepdims=True)
            )
            pool_exp = jnp.where(visible, jnp.exp(pool_scores - peak), 0.0)
            span_exp = jnp.where(causal, jnp.exp(span_scores - peak), 0.0)
            total = jnp.sum(pool_exp, axis=1, keepdims=True) + jnp.sum(span_exp, axis=1, keepdims=True)
            pool_weight = (pool_exp / total).astype(jnp.bfloat16)
            span_weight = (span_exp / total).astype(jnp.bfloat16)
            mixed = jnp.dot(pool_weight, vals, preferred_element_type=jnp.float32) + jnp.dot(
                span_weight, span_vals, preferred_element_type=jnp.float32
            )
            out_ref[:, col : col + HD] = jnp.where(live, mixed, 0.0).astype(jnp.bfloat16)


def vmem_call(kernel, out_shape, operands, flops, transcendentals):
    bytes_accessed = sum(x.size * x.dtype.itemsize for x in operands) + out_shape.size * 2
    return pl.pallas_call(
        kernel,
        out_shape=out_shape,
        in_specs=[pl.BlockSpec(memory_space=pltpu.VMEM)] * len(operands),
        out_specs=pl.BlockSpec(memory_space=pltpu.VMEM),
        cost_estimate=pl.CostEstimate(
            flops=flops, transcendentals=transcendentals, bytes_accessed=bytes_accessed
        ),
    )(*operands)


def term_maker(rows_source, wo):
    return jnp.dot(rows_source, wo, preferred_element_type=jnp.float32)


def per_device(dec_q, dec_kv, dec_owner, dec_table, pre_q, pre_kv, pre_meta, pool, wo):
    groups = lax.axis_size("req")
    tok_rows = dec_q.shape[0]
    capacity = max(2, (2 * tok_rows + groups - 1) // groups)
    slot_count = groups * capacity
    q_width = dec_q.shape[1]
    kv_width = dec_kv.shape[1]

    span_rows = pre_q.shape[0]
    pre_attn = vmem_call(
        prefill_kernel,
        jax.ShapeDtypeStruct((span_rows, q_width), jnp.bfloat16),
        (pre_q, pre_kv, pre_meta, pool),
        4 * span_rows * (pool.shape[0] + span_rows) * q_width,
        span_rows * (pool.shape[0] + span_rows) * q_width // HD,
    )
    pre_part = term_maker(pre_attn, wo).astype(jnp.bfloat16)

    tok_iota = lax.iota(jnp.int32, tok_rows)
    earlier_same = (dec_owner[:, None] == dec_owner[None, :]) & (tok_iota[None, :] < tok_iota[:, None])
    ranking = jnp.sum(earlier_same.astype(jnp.int32), axis=1)
    slot_ids = dec_owner * capacity + ranking
    dispatch = (slot_ids[None, :] == lax.iota(jnp.int32, slot_count)[:, None]).astype(jnp.bfloat16)
    send = (
        jnp.dot(dispatch, jnp.concatenate([dec_q, dec_kv], axis=1), preferred_element_type=jnp.float32)
        .astype(jnp.bfloat16)
        .reshape(groups, capacity, q_width + kv_width)
    )
    recv = lax.all_to_all(send, "req", split_axis=0, concat_axis=0, tiled=True).reshape(
        slot_count, q_width + kv_width
    )
    pre_part, recv = lax.optimization_barrier((pre_part, recv))
    pre_out = lax.psum_scatter(pre_part, "tp", scatter_dimension=0, tiled=True)
    slot_attn = vmem_call(
        decode_kernel,
        jax.ShapeDtypeStruct((slot_count, q_width), jnp.bfloat16),
        (recv, jnp.transpose(dec_table), pool),
        4 * slot_count * pool.shape[0] * q_width,
        slot_count * pool.shape[0] * q_width // HD,
    )
    replies = lax.all_to_all(
        slot_attn.reshape(groups, capacity, q_width), "req", split_axis=0, concat_axis=0, tiled=True
    )
    dec_attn = lax.dot_general(
        dispatch,
        replies.reshape(slot_count, q_width),
        (((0,), (0,)), ((), ())),
        preferred_element_type=jnp.float32,
    ).astype(jnp.bfloat16)
    tp_count = lax.axis_size("tp")
    dec_part = term_maker(dec_attn, wo).astype(jnp.bfloat16)
    pieces = lax.all_to_all(
        dec_part.reshape(tp_count, tok_rows // tp_count, dec_part.shape[1]),
        "tp",
        split_axis=0,
        concat_axis=0,
        tiled=True,
    )
    dec_out = jnp.sum(pieces.astype(jnp.float32), axis=0).astype(jnp.bfloat16)
    return (dec_out, pre_out)


def solution(mesh):
    placed = (
        P("req", "tp"),
        P("req", "tp"),
        P("req"),
        P("req", None),
        P("req", "tp"),
        P("req", "tp"),
        P("req", None),
        P("req", "tp"),
        P("tp", None),
    )
    return jax.shard_map(
        per_device,
        mesh=mesh,
        in_specs=placed,
        out_specs=(P(("req", "tp"), None), P(("req", "tp"), None)),
        check_vma=False,
    )
```

```python
import math

import jax
import jax.numpy as jnp
from jax import lax
from jax.experimental import pallas as pl
from jax.experimental.pallas import tpu as pltpu
from jax.sharding import PartitionSpec as P

HD = 128
QPK = 3


MASKED_SCORE = -1e30


def decode_kernel(recv_ref, table_ref, pool_ref, out_ref):
    score_scale = 1.0 / math.sqrt(HD)
    slot_rows = recv_ref.shape[0] * recv_ref.shape[1]
    recv = recv_ref[...].reshape(slot_rows, recv_ref.shape[2])
    outs = []
    kv_heads = pool_ref.shape[1] // (2 * HD)
    q_width = kv_heads * QPK * HD
    table = table_ref[...]
    spread = jnp.broadcast_to(table[0:1, :], (HD, slot_rows))
    begins = jnp.transpose(spread)[:, 0:1]
    ends = begins + jnp.transpose(jnp.broadcast_to(table[1:2, :], (HD, slot_rows)))[:, 0:1]
    places = lax.broadcasted_iota(jnp.int32, (slot_rows, pool_ref.shape[0]), 1)
    visible = (places >= begins) & (places < ends)
    for g in range(kv_heads):
        keys = pool_ref[:, g * 2 * HD : g * 2 * HD + HD]
        vals = pool_ref[:, g * 2 * HD + HD : (g + 1) * 2 * HD]
        own_key = recv[:, q_width + g * 2 * HD : q_width + g * 2 * HD + HD].astype(jnp.float32)
        own_val = recv[:, q_width + g * 2 * HD + HD : q_width + (g + 1) * 2 * HD].astype(jnp.float32)
        for h in range(QPK):
            col = (g * QPK + h) * HD
            q = recv[:, col : col + HD]
            scores = lax.dot_general(
                q, keys, (((1,), (1,)), ((), ())), preferred_element_type=jnp.float32
            ) * score_scale
            scores = jnp.where(visible, scores, MASKED_SCORE)
            own = jnp.sum(q.astype(jnp.float32) * own_key, axis=1, keepdims=True) * score_scale
            peak = jnp.maximum(jnp.max(scores, axis=1, keepdims=True), own)
            weights = jnp.where(visible, jnp.exp(scores - peak), 0.0)
            own_exp = jnp.exp(own - peak)
            total = jnp.sum(weights, axis=1, keepdims=True) + own_exp
            weights = (weights / total).astype(jnp.bfloat16)
            own_weight = (own_exp / total).astype(jnp.bfloat16).astype(jnp.float32)
            mixed = jnp.dot(weights, vals, preferred_element_type=jnp.float32) + own_weight * own_val
            outs.append(mixed.astype(jnp.bfloat16))
    out_ref[...] = jnp.concatenate(outs, axis=1).reshape(out_ref.shape)


def prefill_kernel(q_ref, kv_ref, meta_ref, pool_ref, out_ref):
    score_scale = 1.0 / math.sqrt(HD)
    span_rows = q_ref.shape[0]
    pool_len = pool_ref.shape[0]
    kv_heads = pool_ref.shape[1] // (2 * HD)
    meta = meta_ref[...]
    begin = meta[:, 0:1]
    end = begin + meta[:, 1:2]
    places = lax.broadcasted_iota(jnp.int32, (span_rows, pool_len), 1)
    visible = (places >= begin) & (places < end)
    row_iota = lax.broadcasted_iota(jnp.int32, (span_rows, span_rows), 0)
    col_iota = lax.broadcasted_iota(jnp.int32, (span_rows, span_rows), 1)
    causal = col_iota <= row_iota
    live = lax.broadcasted_iota(jnp.int32, (span_rows, 1), 0) < meta[:, 2:3]
    for g in range(kv_heads):
        keys = pool_ref[:, g * 2 * HD : g * 2 * HD + HD]
        vals = pool_ref[:, g * 2 * HD + HD : (g + 1) * 2 * HD]
        span_keys = kv_ref[:, g * 2 * HD : g * 2 * HD + HD]
        span_vals = kv_ref[:, g * 2 * HD + HD : (g + 1) * 2 * HD]
        for h in range(QPK):
            col = (g * QPK + h) * HD
            q = q_ref[:, col : col + HD]
            dims = (((1,), (1,)), ((), ()))
            pool_scores = lax.dot_general(q, keys, dims, preferred_element_type=jnp.float32) * score_scale
            pool_scores = jnp.where(visible, pool_scores, MASKED_SCORE)
            span_scores = lax.dot_general(q, span_keys, dims, preferred_element_type=jnp.float32) * score_scale
            span_scores = jnp.where(causal, span_scores, MASKED_SCORE)
            peak = jnp.maximum(
                jnp.max(pool_scores, axis=1, keepdims=True), jnp.max(span_scores, axis=1, keepdims=True)
            )
            pool_exp = jnp.where(visible, jnp.exp(pool_scores - peak), 0.0)
            span_exp = jnp.where(causal, jnp.exp(span_scores - peak), 0.0)
            total = jnp.sum(pool_exp, axis=1, keepdims=True) + jnp.sum(span_exp, axis=1, keepdims=True)
            pool_weight = (pool_exp / total).astype(jnp.bfloat16)
            span_weight = (span_exp / total).astype(jnp.bfloat16)
            mixed = jnp.dot(pool_weight, vals, preferred_element_type=jnp.float32) + jnp.dot(
                span_weight, span_vals, preferred_element_type=jnp.float32
            )
            out_ref[:, col : col + HD] = jnp.where(live, mixed, 0.0).astype(jnp.bfloat16)


def vmem_call(kernel, out_shape, operands, flops, transcendentals):
    bytes_accessed = sum(x.size * x.dtype.itemsize for x in operands) + out_shape.size * 2
    return pl.pallas_call(
        kernel,
        out_shape=out_shape,
        in_specs=[pl.BlockSpec(memory_space=pltpu.VMEM)] * len(operands),
        out_specs=pl.BlockSpec(memory_space=pltpu.VMEM),
        cost_estimate=pl.CostEstimate(
            flops=flops, transcendentals=transcendentals, bytes_accessed=bytes_accessed
        ),
    )(*operands)


def term_maker(rows_source, wo):
    return jnp.dot(rows_source, wo, preferred_element_type=jnp.float32)


def per_device(dec_q, dec_kv, dec_owner, dec_table, pre_q, pre_kv, pre_meta, pool, wo):
    groups = lax.axis_size("req")
    tok_rows = dec_q.shape[0]
    capacity = max(2, (2 * tok_rows + groups - 1) // groups)
    slot_count = groups * capacity
    q_width = dec_q.shape[1]
    kv_width = dec_kv.shape[1]

    span_rows = pre_q.shape[0]
    pre_attn = vmem_call(
        prefill_kernel,
        jax.ShapeDtypeStruct((span_rows, q_width), jnp.bfloat16),
        (pre_q, pre_kv, pre_meta, pool),
        4 * span_rows * (pool.shape[0] + span_rows) * q_width,
        span_rows * (pool.shape[0] + span_rows) * q_width // HD,
    )
    pre_part = term_maker(pre_attn, wo).astype(jnp.bfloat16)

    tok_iota = lax.iota(jnp.int32, tok_rows)
    earlier_same = (dec_owner[:, None] == dec_owner[None, :]) & (tok_iota[None, :] < tok_iota[:, None])
    ranking = jnp.sum(earlier_same.astype(jnp.int32), axis=1)
    slot_ids = dec_owner * capacity + ranking
    dispatch = (slot_ids[None, :] == lax.iota(jnp.int32, slot_count)[:, None]).astype(jnp.bfloat16)
    send = (
        jnp.dot(dispatch, jnp.concatenate([dec_q, dec_kv], axis=1), preferred_element_type=jnp.float32)
        .astype(jnp.bfloat16)
        .reshape(groups, capacity, q_width + kv_width)
    )
    recv = lax.all_to_all(send, "req", split_axis=0, concat_axis=0, tiled=True)
    pre_part, recv = lax.optimization_barrier((pre_part, recv))
    pre_out = lax.psum_scatter(pre_part, "tp", scatter_dimension=0, tiled=True)
    slot_attn = vmem_call(
        decode_kernel,
        jax.ShapeDtypeStruct((groups, capacity, q_width), jnp.bfloat16),
        (recv, jnp.transpose(dec_table), pool),
        4 * slot_count * pool.shape[0] * q_width,
        slot_count * pool.shape[0] * q_width // HD,
    )
    replies = lax.all_to_all(slot_attn, "req", split_axis=0, concat_axis=0, tiled=True)
    dec_attn = lax.dot_general(
        dispatch,
        replies.reshape(slot_count, q_width),
        (((0,), (0,)), ((), ())),
        preferred_element_type=jnp.float32,
    ).astype(jnp.bfloat16)
    tp_count = lax.axis_size("tp")
    dec_part = term_maker(dec_attn, wo).astype(jnp.bfloat16)
    pieces = lax.all_to_all(
        dec_part.reshape(tp_count, tok_rows // tp_count, dec_part.shape[1]),
        "tp",
        split_axis=0,
        concat_axis=0,
        tiled=True,
    )
    dec_out = jnp.sum(pieces.astype(jnp.float32), axis=0).astype(jnp.bfloat16)
    return (dec_out, pre_out)


def solution(mesh):
    placed = (
        P("req", "tp"),
        P("req", "tp"),
        P("req"),
        P("req", None),
        P("req", "tp"),
        P("req", "tp"),
        P("req", None),
        P("req", "tp"),
        P("tp", None),
    )
    return jax.shard_map(
        per_device,
        mesh=mesh,
        in_specs=placed,
        out_specs=(P(("req", "tp"), None), P(("req", "tp"), None)),
        check_vma=False,
    )
```

```python
import math

import jax
import jax.numpy as jnp
from jax import lax
from jax.experimental import pallas as pl
from jax.experimental.pallas import tpu as pltpu
from jax.sharding import PartitionSpec as P

HD = 128
QPK = 3


MASKED_SCORE = -1e30


def decode_kernel(recv_ref, table_ref, pool_ref, out_ref):
    score_scale = 1.0 / math.sqrt(HD)
    slot_rows = recv_ref.shape[0] * recv_ref.shape[1]
    recv = recv_ref[...].reshape(slot_rows, recv_ref.shape[2])
    outs = []
    kv_heads = pool_ref.shape[1] // (2 * HD)
    q_width = kv_heads * QPK * HD
    table = table_ref[...]
    spread = jnp.broadcast_to(table[0:1, :], (HD, slot_rows))
    begins = jnp.transpose(spread)[:, 0:1]
    ends = begins + jnp.transpose(jnp.broadcast_to(table[1:2, :], (HD, slot_rows)))[:, 0:1]
    places = lax.broadcasted_iota(jnp.int32, (slot_rows, pool_ref.shape[0]), 1)
    visible = (places >= begins) & (places < ends)
    for g in range(kv_heads):
        keys = pool_ref[:, g * 2 * HD : g * 2 * HD + HD]
        vals = pool_ref[:, g * 2 * HD + HD : (g + 1) * 2 * HD]
        own_key = recv[:, q_width + g * 2 * HD : q_width + g * 2 * HD + HD].astype(jnp.float32)
        own_val = recv[:, q_width + g * 2 * HD + HD : q_width + (g + 1) * 2 * HD].astype(jnp.float32)
        for h in range(QPK):
            col = (g * QPK + h) * HD
            q = recv[:, col : col + HD]
            scores = lax.dot_general(
                q, keys, (((1,), (1,)), ((), ())), preferred_element_type=jnp.float32
            ) * score_scale
            scores = jnp.where(visible, scores, MASKED_SCORE)
            own = jnp.sum(q.astype(jnp.float32) * own_key, axis=1, keepdims=True) * score_scale
            peak = jnp.maximum(jnp.max(scores, axis=1, keepdims=True), own)
            weights = jnp.where(visible, jnp.exp(scores - peak), 0.0)
            own_exp = jnp.exp(own - peak)
            total = jnp.sum(weights, axis=1, keepdims=True) + own_exp
            weights = (weights / total).astype(jnp.bfloat16)
            own_weight = (own_exp / total).astype(jnp.bfloat16).astype(jnp.float32)
            mixed = jnp.dot(weights, vals, preferred_element_type=jnp.float32) + own_weight * own_val
            outs.append(mixed.astype(jnp.bfloat16))
    out_ref[...] = jnp.concatenate(outs, axis=1).reshape(out_ref.shape)


def prefill_kernel(q_ref, kv_ref, meta_ref, pool_ref, out_ref):
    score_scale = 1.0 / math.sqrt(HD)
    span_rows = q_ref.shape[0]
    pool_len = pool_ref.shape[0]
    kv_heads = pool_ref.shape[1] // (2 * HD)
    meta = meta_ref[...]
    begin = meta[:, 0:1]
    end = begin + meta[:, 1:2]
    places = lax.broadcasted_iota(jnp.int32, (span_rows, pool_len), 1)
    visible = (places >= begin) & (places < end)
    row_iota = lax.broadcasted_iota(jnp.int32, (span_rows, span_rows), 0)
    col_iota = lax.broadcasted_iota(jnp.int32, (span_rows, span_rows), 1)
    causal = col_iota <= row_iota
    live = lax.broadcasted_iota(jnp.int32, (span_rows, 1), 0) < meta[:, 2:3]
    for g in range(kv_heads):
        keys = pool_ref[:, g * 2 * HD : g * 2 * HD + HD]
        vals = pool_ref[:, g * 2 * HD + HD : (g + 1) * 2 * HD]
        span_keys = kv_ref[:, g * 2 * HD : g * 2 * HD + HD]
        span_vals = kv_ref[:, g * 2 * HD + HD : (g + 1) * 2 * HD]
        for h in range(QPK):
            col = (g * QPK + h) * HD
            q = q_ref[:, col : col + HD]
            dims = (((1,), (1,)), ((), ()))
            pool_scores = lax.dot_general(q, keys, dims, preferred_element_type=jnp.float32) * score_scale
            pool_scores = jnp.where(visible, pool_scores, MASKED_SCORE)
            span_scores = lax.dot_general(q, span_keys, dims, preferred_element_type=jnp.float32) * score_scale
            span_scores = jnp.where(causal, span_scores, MASKED_SCORE)
            peak = jnp.maximum(
                jnp.max(pool_scores, axis=1, keepdims=True), jnp.max(span_scores, axis=1, keepdims=True)
            )
            pool_exp = jnp.where(visible, jnp.exp(pool_scores - peak), 0.0)
            span_exp = jnp.where(causal, jnp.exp(span_scores - peak), 0.0)
            total = jnp.sum(pool_exp, axis=1, keepdims=True) + jnp.sum(span_exp, axis=1, keepdims=True)
            pool_weight = (pool_exp / total).astype(jnp.bfloat16)
            span_weight = (span_exp / total).astype(jnp.bfloat16)
            mixed = jnp.dot(pool_weight, vals, preferred_element_type=jnp.float32) + jnp.dot(
                span_weight, span_vals, preferred_element_type=jnp.float32
            )
            out_ref[:, col : col + HD] = jnp.where(live, mixed, 0.0).astype(jnp.bfloat16)


def route_kernel(owner_ref, q_ref, kv_ref, send_ref, dispatch_ref):
    tok_rows = q_ref.shape[0]
    slot_count = dispatch_ref.shape[0]
    capacity = slot_count // send_ref.shape[0]
    owner_row = owner_ref[...]
    owner_col = jnp.transpose(jnp.broadcast_to(owner_row, (tok_rows, tok_rows)))
    earlier = lax.broadcasted_iota(jnp.int32, (tok_rows, tok_rows), 0) < lax.broadcasted_iota(
        jnp.int32, (tok_rows, tok_rows), 1
    )
    same = (owner_col == owner_row) & earlier
    ranking = jnp.sum(same.astype(jnp.int32), axis=0, keepdims=True)
    slot_ids = owner_row * capacity + ranking
    slots = lax.broadcasted_iota(jnp.int32, (slot_count, tok_rows), 0)
    dispatch = (slots == slot_ids).astype(jnp.bfloat16)
    dispatch_ref[...] = dispatch
    rows = jnp.concatenate([q_ref[...], kv_ref[...]], axis=1)
    send = jnp.dot(dispatch, rows, preferred_element_type=jnp.float32).astype(jnp.bfloat16)
    send_ref[...] = send.reshape(send_ref.shape)


def vmem_call(kernel, out_shape, operands, flops, transcendentals):
    bytes_accessed = sum(x.size * x.dtype.itemsize for x in operands) + out_shape.size * 2
    return pl.pallas_call(
        kernel,
        out_shape=out_shape,
        in_specs=[pl.BlockSpec(memory_space=pltpu.VMEM)] * len(operands),
        out_specs=pl.BlockSpec(memory_space=pltpu.VMEM),
        cost_estimate=pl.CostEstimate(
            flops=flops, transcendentals=transcendentals, bytes_accessed=bytes_accessed
        ),
    )(*operands)


def term_maker(rows_source, wo):
    return jnp.dot(rows_source, wo, preferred_element_type=jnp.float32)


def per_device(dec_q, dec_kv, dec_owner, dec_table, pre_q, pre_kv, pre_meta, pool, wo):
    groups = lax.axis_size("req")
    tok_rows = dec_q.shape[0]
    capacity = max(2, (2 * tok_rows + groups - 1) // groups)
    slot_count = groups * capacity
    q_width = dec_q.shape[1]
    kv_width = dec_kv.shape[1]

    span_rows = pre_q.shape[0]
    pre_attn = vmem_call(
        prefill_kernel,
        jax.ShapeDtypeStruct((span_rows, q_width), jnp.bfloat16),
        (pre_q, pre_kv, pre_meta, pool),
        4 * span_rows * (pool.shape[0] + span_rows) * q_width,
        span_rows * (pool.shape[0] + span_rows) * q_width // HD,
    )
    pre_part = term_maker(pre_attn, wo).astype(jnp.bfloat16)

    send, dispatch = pl.pallas_call(
        route_kernel,
        out_shape=(
            jax.ShapeDtypeStruct((groups, capacity, q_width + kv_width), jnp.bfloat16),
            jax.ShapeDtypeStruct((slot_count, tok_rows), jnp.bfloat16),
        ),
        in_specs=[pl.BlockSpec(memory_space=pltpu.VMEM)] * 3,
        out_specs=(pl.BlockSpec(memory_space=pltpu.VMEM), pl.BlockSpec(memory_space=pltpu.VMEM)),
        cost_estimate=pl.CostEstimate(
            flops=2 * slot_count * tok_rows * (q_width + kv_width),
            transcendentals=0,
            bytes_accessed=2 * (tok_rows + slot_count) * (q_width + kv_width),
        ),
    )(dec_owner.reshape(1, tok_rows), dec_q, dec_kv)
    recv = lax.all_to_all(send, "req", split_axis=0, concat_axis=0, tiled=True)
    pre_part, recv = lax.optimization_barrier((pre_part, recv))
    pre_out = lax.psum_scatter(pre_part, "tp", scatter_dimension=0, tiled=True)
    slot_attn = vmem_call(
        decode_kernel,
        jax.ShapeDtypeStruct((groups, capacity, q_width), jnp.bfloat16),
        (recv, jnp.transpose(dec_table), pool),
        4 * slot_count * pool.shape[0] * q_width,
        slot_count * pool.shape[0] * q_width // HD,
    )
    replies = lax.all_to_all(slot_attn, "req", split_axis=0, concat_axis=0, tiled=True)
    dec_attn = lax.dot_general(
        dispatch,
        replies.reshape(slot_count, q_width),
        (((0,), (0,)), ((), ())),
        preferred_element_type=jnp.float32,
    ).astype(jnp.bfloat16)
    tp_count = lax.axis_size("tp")
    dec_part = term_maker(dec_attn, wo).astype(jnp.bfloat16)
    pieces = lax.all_to_all(
        dec_part.reshape(tp_count, tok_rows // tp_count, dec_part.shape[1]),
        "tp",
        split_axis=0,
        concat_axis=0,
        tiled=True,
    )
    dec_out = jnp.sum(pieces.astype(jnp.float32), axis=0).astype(jnp.bfloat16)
    return (dec_out, pre_out)


def solution(mesh):
    placed = (
        P("req", "tp"),
        P("req", "tp"),
        P("req"),
        P("req", None),
        P("req", "tp"),
        P("req", "tp"),
        P("req", None),
        P("req", "tp"),
        P("tp", None),
    )
    return jax.shard_map(
        per_device,
        mesh=mesh,
        in_specs=placed,
        out_specs=(P(("req", "tp"), None), P(("req", "tp"), None)),
        check_vma=False,
    )
```

```python
import math

import jax
import jax.numpy as jnp
from jax import lax
from jax.experimental import pallas as pl
from jax.experimental.pallas import tpu as pltpu
from jax.sharding import PartitionSpec as P

HD = 128
QPK = 3


MASKED_SCORE = -1e30


def decode_kernel(recv_ref, table_ref, pool_ref, out_ref):
    score_scale = 1.0 / math.sqrt(HD)
    slot_rows = recv_ref.shape[0] * recv_ref.shape[1]
    recv = recv_ref[...].reshape(slot_rows, recv_ref.shape[2])
    outs = []
    kv_heads = pool_ref.shape[1] // (2 * HD)
    q_width = kv_heads * QPK * HD
    table = table_ref[...]
    spread = jnp.broadcast_to(table[0:1, :], (HD, slot_rows))
    begins = jnp.transpose(spread)[:, 0:1]
    ends = begins + jnp.transpose(jnp.broadcast_to(table[1:2, :], (HD, slot_rows)))[:, 0:1]
    places = lax.broadcasted_iota(jnp.int32, (slot_rows, pool_ref.shape[0]), 1)
    visible = (places >= begins) & (places < ends)
    for g in range(kv_heads):
        keys = pool_ref[:, g * 2 * HD : g * 2 * HD + HD]
        vals = pool_ref[:, g * 2 * HD + HD : (g + 1) * 2 * HD]
        own_key = recv[:, q_width + g * 2 * HD : q_width + g * 2 * HD + HD].astype(jnp.float32)
        own_val = recv[:, q_width + g * 2 * HD + HD : q_width + (g + 1) * 2 * HD].astype(jnp.float32)
        for h in range(QPK):
            col = (g * QPK + h) * HD
            q = recv[:, col : col + HD]
            scores = lax.dot_general(
                q, keys, (((1,), (1,)), ((), ())), preferred_element_type=jnp.float32
            ) * score_scale
            scores = jnp.where(visible, scores, MASKED_SCORE)
            own = jnp.sum(q.astype(jnp.float32) * own_key, axis=1, keepdims=True) * score_scale
            peak = jnp.maximum(jnp.max(scores, axis=1, keepdims=True), own)
            weights = jnp.exp(scores - peak)
            own_exp = jnp.exp(own - peak)
            total = jnp.sum(weights, axis=1, keepdims=True) + own_exp
            inverse = 1.0 / total
            weights = (weights * inverse).astype(jnp.bfloat16)
            own_weight = (own_exp * inverse).astype(jnp.bfloat16).astype(jnp.float32)
            mixed = jnp.dot(weights, vals, preferred_element_type=jnp.float32) + own_weight * own_val
            outs.append(mixed.astype(jnp.bfloat16))
    out_ref[...] = jnp.concatenate(outs, axis=1).reshape(out_ref.shape)


def prefill_kernel(q_ref, kv_ref, meta_ref, pool_ref, out_ref):
    score_scale = 1.0 / math.sqrt(HD)
    span_rows = q_ref.shape[0]
    pool_len = pool_ref.shape[0]
    kv_heads = pool_ref.shape[1] // (2 * HD)
    meta = meta_ref[...]
    begin = meta[:, 0:1]
    end = begin + meta[:, 1:2]
    places = lax.broadcasted_iota(jnp.int32, (span_rows, pool_len), 1)
    visible = (places >= begin) & (places < end)
    row_iota = lax.broadcasted_iota(jnp.int32, (span_rows, span_rows), 0)
    col_iota = lax.broadcasted_iota(jnp.int32, (span_rows, span_rows), 1)
    causal = col_iota <= row_iota
    live = lax.broadcasted_iota(jnp.int32, (span_rows, 1), 0) < meta[:, 2:3]
    for g in range(kv_heads):
        keys = pool_ref[:, g * 2 * HD : g * 2 * HD + HD]
        vals = pool_ref[:, g * 2 * HD + HD : (g + 1) * 2 * HD]
        span_keys = kv_ref[:, g * 2 * HD : g * 2 * HD + HD]
        span_vals = kv_ref[:, g * 2 * HD + HD : (g + 1) * 2 * HD]
        for h in range(QPK):
            col = (g * QPK + h) * HD
            q = q_ref[:, col : col + HD]
            dims = (((1,), (1,)), ((), ()))
            pool_scores = lax.dot_general(q, keys, dims, preferred_element_type=jnp.float32) * score_scale
            pool_scores = jnp.where(visible, pool_scores, MASKED_SCORE)
            span_scores = lax.dot_general(q, span_keys, dims, preferred_element_type=jnp.float32) * score_scale
            span_scores = jnp.where(causal, span_scores, MASKED_SCORE)
            peak = jnp.maximum(
                jnp.max(pool_scores, axis=1, keepdims=True), jnp.max(span_scores, axis=1, keepdims=True)
            )
            pool_exp = jnp.where(visible, jnp.exp(pool_scores - peak), 0.0)
            span_exp = jnp.where(causal, jnp.exp(span_scores - peak), 0.0)
            total = jnp.sum(pool_exp, axis=1, keepdims=True) + jnp.sum(span_exp, axis=1, keepdims=True)
            pool_weight = (pool_exp / total).astype(jnp.bfloat16)
            span_weight = (span_exp / total).astype(jnp.bfloat16)
            mixed = jnp.dot(pool_weight, vals, preferred_element_type=jnp.float32) + jnp.dot(
                span_weight, span_vals, preferred_element_type=jnp.float32
            )
            out_ref[:, col : col + HD] = jnp.where(live, mixed, 0.0).astype(jnp.bfloat16)


def route_kernel(owner_ref, q_ref, kv_ref, send_ref, dispatch_ref):
    tok_rows = q_ref.shape[0]
    slot_count = dispatch_ref.shape[0]
    capacity = slot_count // send_ref.shape[0]
    owner_row = owner_ref[...]
    owner_col = jnp.transpose(jnp.broadcast_to(owner_row, (tok_rows, tok_rows)))
    earlier = lax.broadcasted_iota(jnp.int32, (tok_rows, tok_rows), 0) < lax.broadcasted_iota(
        jnp.int32, (tok_rows, tok_rows), 1
    )
    same = (owner_col == owner_row) & earlier
    ranking = jnp.sum(same.astype(jnp.int32), axis=0, keepdims=True)
    slot_ids = owner_row * capacity + ranking
    slots = lax.broadcasted_iota(jnp.int32, (slot_count, tok_rows), 0)
    dispatch = (slots == slot_ids).astype(jnp.bfloat16)
    dispatch_ref[...] = dispatch
    rows = jnp.concatenate([q_ref[...], kv_ref[...]], axis=1)
    send = jnp.dot(dispatch, rows, preferred_element_type=jnp.float32).astype(jnp.bfloat16)
    send_ref[...] = send.reshape(send_ref.shape)


def vmem_call(kernel, out_shape, operands, flops, transcendentals):
    bytes_accessed = sum(x.size * x.dtype.itemsize for x in operands) + out_shape.size * 2
    return pl.pallas_call(
        kernel,
        out_shape=out_shape,
        in_specs=[pl.BlockSpec(memory_space=pltpu.VMEM)] * len(operands),
        out_specs=pl.BlockSpec(memory_space=pltpu.VMEM),
        cost_estimate=pl.CostEstimate(
            flops=flops, transcendentals=transcendentals, bytes_accessed=bytes_accessed
        ),
    )(*operands)


def term_maker(rows_source, wo):
    return jnp.dot(rows_source, wo, preferred_element_type=jnp.float32)


def per_device(dec_q, dec_kv, dec_owner, dec_table, pre_q, pre_kv, pre_meta, pool, wo):
    groups = lax.axis_size("req")
    tok_rows = dec_q.shape[0]
    capacity = max(2, (2 * tok_rows + groups - 1) // groups)
    slot_count = groups * capacity
    q_width = dec_q.shape[1]
    kv_width = dec_kv.shape[1]

    span_rows = pre_q.shape[0]
    pre_attn = vmem_call(
        prefill_kernel,
        jax.ShapeDtypeStruct((span_rows, q_width), jnp.bfloat16),
        (pre_q, pre_kv, pre_meta, pool),
        4 * span_rows * (pool.shape[0] + span_rows) * q_width,
        span_rows * (pool.shape[0] + span_rows) * q_width // HD,
    )
    pre_part = term_maker(pre_attn, wo).astype(jnp.bfloat16)

    send, dispatch = pl.pallas_call(
        route_kernel,
        out_shape=(
            jax.ShapeDtypeStruct((groups, capacity, q_width + kv_width), jnp.bfloat16),
            jax.ShapeDtypeStruct((slot_count, tok_rows), jnp.bfloat16),
        ),
        in_specs=[pl.BlockSpec(memory_space=pltpu.VMEM)] * 3,
        out_specs=(pl.BlockSpec(memory_space=pltpu.VMEM), pl.BlockSpec(memory_space=pltpu.VMEM)),
        cost_estimate=pl.CostEstimate(
            flops=2 * slot_count * tok_rows * (q_width + kv_width),
            transcendentals=0,
            bytes_accessed=2 * (tok_rows + slot_count) * (q_width + kv_width),
        ),
    )(dec_owner.reshape(1, tok_rows), dec_q, dec_kv)
    recv = lax.all_to_all(send, "req", split_axis=0, concat_axis=0, tiled=True)
    pre_part, recv = lax.optimization_barrier((pre_part, recv))
    pre_out = lax.psum_scatter(pre_part, "tp", scatter_dimension=0, tiled=True)
    slot_attn = vmem_call(
        decode_kernel,
        jax.ShapeDtypeStruct((groups, capacity, q_width), jnp.bfloat16),
        (recv, jnp.transpose(dec_table), pool),
        4 * slot_count * pool.shape[0] * q_width,
        slot_count * pool.shape[0] * q_width // HD,
    )
    replies = lax.all_to_all(slot_attn, "req", split_axis=0, concat_axis=0, tiled=True)
    dec_attn = lax.dot_general(
        dispatch,
        replies.reshape(slot_count, q_width),
        (((0,), (0,)), ((), ())),
        preferred_element_type=jnp.float32,
    ).astype(jnp.bfloat16)
    tp_count = lax.axis_size("tp")
    dec_part = term_maker(dec_attn, wo).astype(jnp.bfloat16)
    pieces = lax.all_to_all(
        dec_part.reshape(tp_count, tok_rows // tp_count, dec_part.shape[1]),
        "tp",
        split_axis=0,
        concat_axis=0,
        tiled=True,
    )
    dec_out = jnp.sum(pieces.astype(jnp.float32), axis=0).astype(jnp.bfloat16)
    return (dec_out, pre_out)


def solution(mesh):
    placed = (
        P("req", "tp"),
        P("req", "tp"),
        P("req"),
        P("req", None),
        P("req", "tp"),
        P("req", "tp"),
        P("req", None),
        P("req", "tp"),
        P("tp", None),
    )
    return jax.shard_map(
        per_device,
        mesh=mesh,
        in_specs=placed,
        out_specs=(P(("req", "tp"), None), P(("req", "tp"), None)),
        check_vma=False,
    )
```

```python
import math

import jax
import jax.numpy as jnp
from jax import lax
from jax.experimental import pallas as pl
from jax.experimental.pallas import tpu as pltpu
from jax.sharding import PartitionSpec as P

HD = 128
QPK = 3


MASKED_SCORE = -1e30


def decode_kernel(recv_ref, table_ref, pool_ref, out_ref):
    score_scale = 1.0 / math.sqrt(HD)
    slot_rows = recv_ref.shape[0] * recv_ref.shape[1]
    recv = recv_ref[...].reshape(slot_rows, recv_ref.shape[2])
    outs = []
    kv_heads = pool_ref.shape[1] // (2 * HD)
    q_width = kv_heads * QPK * HD
    table = table_ref[...]
    spread = jnp.broadcast_to(table[0:1, :], (HD, slot_rows))
    begins = jnp.transpose(spread)[:, 0:1]
    ends = begins + jnp.transpose(jnp.broadcast_to(table[1:2, :], (HD, slot_rows)))[:, 0:1]
    places = lax.broadcasted_iota(jnp.int32, (slot_rows, pool_ref.shape[0]), 1)
    visible = (places >= begins) & (places < ends)
    for g in range(kv_heads):
        keys = pool_ref[:, g * 2 * HD : g * 2 * HD + HD]
        vals = pool_ref[:, g * 2 * HD + HD : (g + 1) * 2 * HD]
        own_key = recv[:, q_width + g * 2 * HD : q_width + g * 2 * HD + HD].astype(jnp.float32)
        own_val = recv[:, q_width + g * 2 * HD + HD : q_width + (g + 1) * 2 * HD].astype(jnp.float32)
        first = g * QPK * HD
        q = jnp.concatenate(
            [recv[:, first + h * HD : first + (h + 1) * HD] for h in range(QPK)], axis=0
        )
        own_key = jnp.concatenate([own_key] * QPK, axis=0)
        own_val = jnp.concatenate([own_val] * QPK, axis=0)
        seen = jnp.concatenate([visible] * QPK, axis=0)
        scores = lax.dot_general(
            q, keys, (((1,), (1,)), ((), ())), preferred_element_type=jnp.float32
        ) * score_scale
        scores = jnp.where(seen, scores, MASKED_SCORE)
        own = jnp.sum(q.astype(jnp.float32) * own_key, axis=1, keepdims=True) * score_scale
        peak = jnp.maximum(jnp.max(scores, axis=1, keepdims=True), own)
        weights = jnp.where(seen, jnp.exp(scores - peak), 0.0)
        own_exp = jnp.exp(own - peak)
        total = jnp.sum(weights, axis=1, keepdims=True) + own_exp
        weights = (weights / total).astype(jnp.bfloat16)
        own_weight = (own_exp / total).astype(jnp.bfloat16).astype(jnp.float32)
        mixed = jnp.dot(weights, vals, preferred_element_type=jnp.float32) + own_weight * own_val
        mixed = mixed.astype(jnp.bfloat16)
        outs.extend(mixed[h * slot_rows : (h + 1) * slot_rows] for h in range(QPK))
    out_ref[...] = jnp.concatenate(outs, axis=1).reshape(out_ref.shape)


def prefill_kernel(q_ref, kv_ref, meta_ref, pool_ref, out_ref):
    score_scale = 1.0 / math.sqrt(HD)
    span_rows = q_ref.shape[0]
    pool_len = pool_ref.shape[0]
    kv_heads = pool_ref.shape[1] // (2 * HD)
    meta = meta_ref[...]
    begin = meta[:, 0:1]
    end = begin + meta[:, 1:2]
    places = lax.broadcasted_iota(jnp.int32, (span_rows, pool_len), 1)
    visible = (places >= begin) & (places < end)
    row_iota = lax.broadcasted_iota(jnp.int32, (span_rows, span_rows), 0)
    col_iota = lax.broadcasted_iota(jnp.int32, (span_rows, span_rows), 1)
    causal = col_iota <= row_iota
    live = lax.broadcasted_iota(jnp.int32, (span_rows, 1), 0) < meta[:, 2:3]
    for g in range(kv_heads):
        keys = pool_ref[:, g * 2 * HD : g * 2 * HD + HD]
        vals = pool_ref[:, g * 2 * HD + HD : (g + 1) * 2 * HD]
        span_keys = kv_ref[:, g * 2 * HD : g * 2 * HD + HD]
        span_vals = kv_ref[:, g * 2 * HD + HD : (g + 1) * 2 * HD]
        for h in range(QPK):
            col = (g * QPK + h) * HD
            q = q_ref[:, col : col + HD]
            dims = (((1,), (1,)), ((), ()))
            pool_scores = lax.dot_general(q, keys, dims, preferred_element_type=jnp.float32) * score_scale
            pool_scores = jnp.where(visible, pool_scores, MASKED_SCORE)
            span_scores = lax.dot_general(q, span_keys, dims, preferred_element_type=jnp.float32) * score_scale
            span_scores = jnp.where(causal, span_scores, MASKED_SCORE)
            peak = jnp.maximum(
                jnp.max(pool_scores, axis=1, keepdims=True), jnp.max(span_scores, axis=1, keepdims=True)
            )
            pool_exp = jnp.where(visible, jnp.exp(pool_scores - peak), 0.0)
            span_exp = jnp.where(causal, jnp.exp(span_scores - peak), 0.0)
            total = jnp.sum(pool_exp, axis=1, keepdims=True) + jnp.sum(span_exp, axis=1, keepdims=True)
            pool_weight = (pool_exp / total).astype(jnp.bfloat16)
            span_weight = (span_exp / total).astype(jnp.bfloat16)
            mixed = jnp.dot(pool_weight, vals, preferred_element_type=jnp.float32) + jnp.dot(
                span_weight, span_vals, preferred_element_type=jnp.float32
            )
            out_ref[:, col : col + HD] = jnp.where(live, mixed, 0.0).astype(jnp.bfloat16)


def route_kernel(owner_ref, q_ref, kv_ref, send_ref, dispatch_ref):
    tok_rows = q_ref.shape[0]
    slot_count = dispatch_ref.shape[0]
    capacity = slot_count // send_ref.shape[0]
    owner_row = owner_ref[...]
    owner_col = jnp.transpose(jnp.broadcast_to(owner_row, (tok_rows, tok_rows)))
    earlier = lax.broadcasted_iota(jnp.int32, (tok_rows, tok_rows), 0) < lax.broadcasted_iota(
        jnp.int32, (tok_rows, tok_rows), 1
    )
    same = (owner_col == owner_row) & earlier
    ranking = jnp.sum(same.astype(jnp.int32), axis=0, keepdims=True)
    slot_ids = owner_row * capacity + ranking
    slots = lax.broadcasted_iota(jnp.int32, (slot_count, tok_rows), 0)
    dispatch = (slots == slot_ids).astype(jnp.bfloat16)
    dispatch_ref[...] = dispatch
    rows = jnp.concatenate([q_ref[...], kv_ref[...]], axis=1)
    send = jnp.dot(dispatch, rows, preferred_element_type=jnp.float32).astype(jnp.bfloat16)
    send_ref[...] = send.reshape(send_ref.shape)


def vmem_call(kernel, out_shape, operands, flops, transcendentals):
    bytes_accessed = sum(x.size * x.dtype.itemsize for x in operands) + out_shape.size * 2
    return pl.pallas_call(
        kernel,
        out_shape=out_shape,
        in_specs=[pl.BlockSpec(memory_space=pltpu.VMEM)] * len(operands),
        out_specs=pl.BlockSpec(memory_space=pltpu.VMEM),
        cost_estimate=pl.CostEstimate(
            flops=flops, transcendentals=transcendentals, bytes_accessed=bytes_accessed
        ),
    )(*operands)


def term_maker(rows_source, wo):
    return jnp.dot(rows_source, wo, preferred_element_type=jnp.float32)


def per_device(dec_q, dec_kv, dec_owner, dec_table, pre_q, pre_kv, pre_meta, pool, wo):
    groups = lax.axis_size("req")
    tok_rows = dec_q.shape[0]
    capacity = max(2, (2 * tok_rows + groups - 1) // groups)
    slot_count = groups * capacity
    q_width = dec_q.shape[1]
    kv_width = dec_kv.shape[1]

    span_rows = pre_q.shape[0]
    pre_attn = vmem_call(
        prefill_kernel,
        jax.ShapeDtypeStruct((span_rows, q_width), jnp.bfloat16),
        (pre_q, pre_kv, pre_meta, pool),
        4 * span_rows * (pool.shape[0] + span_rows) * q_width,
        span_rows * (pool.shape[0] + span_rows) * q_width // HD,
    )
    pre_part = term_maker(pre_attn, wo).astype(jnp.bfloat16)

    send, dispatch = pl.pallas_call(
        route_kernel,
        out_shape=(
            jax.ShapeDtypeStruct((groups, capacity, q_width + kv_width), jnp.bfloat16),
            jax.ShapeDtypeStruct((slot_count, tok_rows), jnp.bfloat16),
        ),
        in_specs=[pl.BlockSpec(memory_space=pltpu.VMEM)] * 3,
        out_specs=(pl.BlockSpec(memory_space=pltpu.VMEM), pl.BlockSpec(memory_space=pltpu.VMEM)),
        cost_estimate=pl.CostEstimate(
            flops=2 * slot_count * tok_rows * (q_width + kv_width),
            transcendentals=0,
            bytes_accessed=2 * (tok_rows + slot_count) * (q_width + kv_width),
        ),
    )(dec_owner.reshape(1, tok_rows), dec_q, dec_kv)
    recv = lax.all_to_all(send, "req", split_axis=0, concat_axis=0, tiled=True)
    pre_part, recv = lax.optimization_barrier((pre_part, recv))
    pre_out = lax.psum_scatter(pre_part, "tp", scatter_dimension=0, tiled=True)
    slot_attn = vmem_call(
        decode_kernel,
        jax.ShapeDtypeStruct((groups, capacity, q_width), jnp.bfloat16),
        (recv, jnp.transpose(dec_table), pool),
        4 * slot_count * pool.shape[0] * q_width,
        slot_count * pool.shape[0] * q_width // HD,
    )
    replies = lax.all_to_all(slot_attn, "req", split_axis=0, concat_axis=0, tiled=True)
    dec_attn = lax.dot_general(
        dispatch,
        replies.reshape(slot_count, q_width),
        (((0,), (0,)), ((), ())),
        preferred_element_type=jnp.float32,
    ).astype(jnp.bfloat16)
    tp_count = lax.axis_size("tp")
    dec_part = term_maker(dec_attn, wo).astype(jnp.bfloat16)
    pieces = lax.all_to_all(
        dec_part.reshape(tp_count, tok_rows // tp_count, dec_part.shape[1]),
        "tp",
        split_axis=0,
        concat_axis=0,
        tiled=True,
    )
    dec_out = jnp.sum(pieces.astype(jnp.float32), axis=0).astype(jnp.bfloat16)
    return (dec_out, pre_out)


def solution(mesh):
    placed = (
        P("req", "tp"),
        P("req", "tp"),
        P("req"),
        P("req", None),
        P("req", "tp"),
        P("req", "tp"),
        P("req", None),
        P("req", "tp"),
        P("tp", None),
    )
    return jax.shard_map(
        per_device,
        mesh=mesh,
        in_specs=placed,
        out_specs=(P(("req", "tp"), None), P(("req", "tp"), None)),
        check_vma=False,
    )
```

```python
import math

import jax
import jax.numpy as jnp
from jax import lax
from jax.experimental import pallas as pl
from jax.experimental.pallas import tpu as pltpu
from jax.sharding import PartitionSpec as P

HD = 128
QPK = 3


MASKED_SCORE = -1e30


def decode_kernel(recv_ref, table_ref, pool_ref, keys_t_ref, out_ref):
    score_scale = 1.0 / math.sqrt(HD)
    slot_rows = recv_ref.shape[0] * recv_ref.shape[1]
    recv = recv_ref[...].reshape(slot_rows, recv_ref.shape[2])
    outs = []
    kv_heads = pool_ref.shape[1] // (2 * HD)
    q_width = kv_heads * QPK * HD
    table = table_ref[...]
    spread = jnp.broadcast_to(table[0:1, :], (HD, slot_rows))
    begins = jnp.transpose(spread)[:, 0:1]
    ends = begins + jnp.transpose(jnp.broadcast_to(table[1:2, :], (HD, slot_rows)))[:, 0:1]
    places = lax.broadcasted_iota(jnp.int32, (slot_rows, pool_ref.shape[0]), 1)
    visible = (places >= begins) & (places < ends)
    for g in range(kv_heads):
        keys_t = keys_t_ref[g * HD : (g + 1) * HD, :]
        vals = pool_ref[:, g * 2 * HD + HD : (g + 1) * 2 * HD]
        own_key = recv[:, q_width + g * 2 * HD : q_width + g * 2 * HD + HD].astype(jnp.float32)
        own_val = recv[:, q_width + g * 2 * HD + HD : q_width + (g + 1) * 2 * HD].astype(jnp.float32)
        for h in range(QPK):
            col = (g * QPK + h) * HD
            q = recv[:, col : col + HD]
            scores = jnp.dot(q, keys_t, preferred_element_type=jnp.float32) * score_scale
            scores = jnp.where(visible, scores, MASKED_SCORE)
            own = jnp.sum(q.astype(jnp.float32) * own_key, axis=1, keepdims=True) * score_scale
            peak = jnp.maximum(jnp.max(scores, axis=1, keepdims=True), own)
            weights = jnp.where(visible, jnp.exp(scores - peak), 0.0)
            own_exp = jnp.exp(own - peak)
            total = jnp.sum(weights, axis=1, keepdims=True) + own_exp
            weights = (weights / total).astype(jnp.bfloat16)
            own_weight = (own_exp / total).astype(jnp.bfloat16).astype(jnp.float32)
            mixed = jnp.dot(weights, vals, preferred_element_type=jnp.float32) + own_weight * own_val
            outs.append(mixed.astype(jnp.bfloat16))
    out_ref[...] = jnp.concatenate(outs, axis=1).reshape(out_ref.shape)


def prefill_kernel(q_ref, kv_ref, meta_ref, pool_ref, out_ref, keys_t_ref):
    score_scale = 1.0 / math.sqrt(HD)
    span_rows = q_ref.shape[0]
    pool_len = pool_ref.shape[0]
    kv_heads = pool_ref.shape[1] // (2 * HD)
    meta = meta_ref[...]
    begin = meta[:, 0:1]
    end = begin + meta[:, 1:2]
    places = lax.broadcasted_iota(jnp.int32, (span_rows, pool_len), 1)
    visible = (places >= begin) & (places < end)
    row_iota = lax.broadcasted_iota(jnp.int32, (span_rows, span_rows), 0)
    col_iota = lax.broadcasted_iota(jnp.int32, (span_rows, span_rows), 1)
    causal = col_iota <= row_iota
    live = lax.broadcasted_iota(jnp.int32, (span_rows, 1), 0) < meta[:, 2:3]
    for g in range(kv_heads):
        keys = pool_ref[:, g * 2 * HD : g * 2 * HD + HD]
        keys_t_ref[g * HD : (g + 1) * HD, :] = jnp.transpose(keys)
        vals = pool_ref[:, g * 2 * HD + HD : (g + 1) * 2 * HD]
        span_keys = kv_ref[:, g * 2 * HD : g * 2 * HD + HD]
        span_vals = kv_ref[:, g * 2 * HD + HD : (g + 1) * 2 * HD]
        for h in range(QPK):
            col = (g * QPK + h) * HD
            q = q_ref[:, col : col + HD]
            dims = (((1,), (1,)), ((), ()))
            pool_scores = lax.dot_general(q, keys, dims, preferred_element_type=jnp.float32) * score_scale
            pool_scores = jnp.where(visible, pool_scores, MASKED_SCORE)
            span_scores = lax.dot_general(q, span_keys, dims, preferred_element_type=jnp.float32) * score_scale
            span_scores = jnp.where(causal, span_scores, MASKED_SCORE)
            peak = jnp.maximum(
                jnp.max(pool_scores, axis=1, keepdims=True), jnp.max(span_scores, axis=1, keepdims=True)
            )
            pool_exp = jnp.where(visible, jnp.exp(pool_scores - peak), 0.0)
            span_exp = jnp.where(causal, jnp.exp(span_scores - peak), 0.0)
            total = jnp.sum(pool_exp, axis=1, keepdims=True) + jnp.sum(span_exp, axis=1, keepdims=True)
            pool_weight = (pool_exp / total).astype(jnp.bfloat16)
            span_weight = (span_exp / total).astype(jnp.bfloat16)
            mixed = jnp.dot(pool_weight, vals, preferred_element_type=jnp.float32) + jnp.dot(
                span_weight, span_vals, preferred_element_type=jnp.float32
            )
            out_ref[:, col : col + HD] = jnp.where(live, mixed, 0.0).astype(jnp.bfloat16)


def route_kernel(owner_ref, q_ref, kv_ref, send_ref, dispatch_ref):
    tok_rows = q_ref.shape[0]
    slot_count = dispatch_ref.shape[0]
    capacity = slot_count // send_ref.shape[0]
    owner_row = owner_ref[...]
    owner_col = jnp.transpose(jnp.broadcast_to(owner_row, (tok_rows, tok_rows)))
    earlier = lax.broadcasted_iota(jnp.int32, (tok_rows, tok_rows), 0) < lax.broadcasted_iota(
        jnp.int32, (tok_rows, tok_rows), 1
    )
    same = (owner_col == owner_row) & earlier
    ranking = jnp.sum(same.astype(jnp.int32), axis=0, keepdims=True)
    slot_ids = owner_row * capacity + ranking
    slots = lax.broadcasted_iota(jnp.int32, (slot_count, tok_rows), 0)
    dispatch = (slots == slot_ids).astype(jnp.bfloat16)
    dispatch_ref[...] = dispatch
    rows = jnp.concatenate([q_ref[...], kv_ref[...]], axis=1)
    send = jnp.dot(dispatch, rows, preferred_element_type=jnp.float32).astype(jnp.bfloat16)
    send_ref[...] = send.reshape(send_ref.shape)


def vmem_call(kernel, out_shape, operands, flops, transcendentals):
    bytes_accessed = sum(x.size * x.dtype.itemsize for x in operands) + out_shape.size * 2
    return pl.pallas_call(
        kernel,
        out_shape=out_shape,
        in_specs=[pl.BlockSpec(memory_space=pltpu.VMEM)] * len(operands),
        out_specs=pl.BlockSpec(memory_space=pltpu.VMEM),
        cost_estimate=pl.CostEstimate(
            flops=flops, transcendentals=transcendentals, bytes_accessed=bytes_accessed
        ),
    )(*operands)


def term_maker(rows_source, wo):
    return jnp.dot(rows_source, wo, preferred_element_type=jnp.float32)


def per_device(dec_q, dec_kv, dec_owner, dec_table, pre_q, pre_kv, pre_meta, pool, wo):
    groups = lax.axis_size("req")
    tok_rows = dec_q.shape[0]
    capacity = max(2, (2 * tok_rows + groups - 1) // groups)
    slot_count = groups * capacity
    q_width = dec_q.shape[1]
    kv_width = dec_kv.shape[1]

    span_rows = pre_q.shape[0]
    kv_heads = pool.shape[1] // (2 * HD)
    pre_attn, keys_t = pl.pallas_call(
        prefill_kernel,
        out_shape=(
            jax.ShapeDtypeStruct((span_rows, q_width), jnp.bfloat16),
            jax.ShapeDtypeStruct((kv_heads * HD, pool.shape[0]), jnp.bfloat16),
        ),
        in_specs=[pl.BlockSpec(memory_space=pltpu.VMEM)] * 4,
        out_specs=(pl.BlockSpec(memory_space=pltpu.VMEM), pl.BlockSpec(memory_space=pltpu.VMEM)),
        cost_estimate=pl.CostEstimate(
            flops=4 * span_rows * (pool.shape[0] + span_rows) * q_width,
            transcendentals=span_rows * (pool.shape[0] + span_rows) * q_width // HD,
            bytes_accessed=2 * (pre_q.size + pre_kv.size + pool.size + span_rows * q_width),
        ),
    )(pre_q, pre_kv, pre_meta, pool)
    pre_part = term_maker(pre_attn, wo).astype(jnp.bfloat16)

    send, dispatch = pl.pallas_call(
        route_kernel,
        out_shape=(
            jax.ShapeDtypeStruct((groups, capacity, q_width + kv_width), jnp.bfloat16),
            jax.ShapeDtypeStruct((slot_count, tok_rows), jnp.bfloat16),
        ),
        in_specs=[pl.BlockSpec(memory_space=pltpu.VMEM)] * 3,
        out_specs=(pl.BlockSpec(memory_space=pltpu.VMEM), pl.BlockSpec(memory_space=pltpu.VMEM)),
        cost_estimate=pl.CostEstimate(
            flops=2 * slot_count * tok_rows * (q_width + kv_width),
            transcendentals=0,
            bytes_accessed=2 * (tok_rows + slot_count) * (q_width + kv_width),
        ),
    )(dec_owner.reshape(1, tok_rows), dec_q, dec_kv)
    recv = lax.all_to_all(send, "req", split_axis=0, concat_axis=0, tiled=True)
    pre_part, recv = lax.optimization_barrier((pre_part, recv))
    pre_out = lax.psum_scatter(pre_part, "tp", scatter_dimension=0, tiled=True)
    slot_attn = vmem_call(
        decode_kernel,
        jax.ShapeDtypeStruct((groups, capacity, q_width), jnp.bfloat16),
        (recv, jnp.transpose(dec_table), pool, keys_t),
        4 * slot_count * pool.shape[0] * q_width,
        slot_count * pool.shape[0] * q_width // HD,
    )
    replies = lax.all_to_all(slot_attn, "req", split_axis=0, concat_axis=0, tiled=True)
    dec_attn = lax.dot_general(
        dispatch,
        replies.reshape(slot_count, q_width),
        (((0,), (0,)), ((), ())),
        preferred_element_type=jnp.float32,
    ).astype(jnp.bfloat16)
    tp_count = lax.axis_size("tp")
    dec_part = term_maker(dec_attn, wo).astype(jnp.bfloat16)
    pieces = lax.all_to_all(
        dec_part.reshape(tp_count, tok_rows // tp_count, dec_part.shape[1]),
        "tp",
        split_axis=0,
        concat_axis=0,
        tiled=True,
    )
    dec_out = jnp.sum(pieces.astype(jnp.float32), axis=0).astype(jnp.bfloat16)
    return (dec_out, pre_out)


def solution(mesh):
    placed = (
        P("req", "tp"),
        P("req", "tp"),
        P("req"),
        P("req", None),
        P("req", "tp"),
        P("req", "tp"),
        P("req", None),
        P("req", "tp"),
        P("tp", None),
    )
    return jax.shard_map(
        per_device,
        mesh=mesh,
        in_specs=placed,
        out_specs=(P(("req", "tp"), None), P(("req", "tp"), None)),
        check_vma=False,
    )
```

```python
import math

import jax
import jax.numpy as jnp
from jax import lax
from jax.experimental import pallas as pl
from jax.experimental.pallas import tpu as pltpu
from jax.sharding import PartitionSpec as P

HD = 128
QPK = 3


MASKED_SCORE = -1e30


def decode_kernel(recv_ref, table_ref, pool_ref, out_ref):
    score_scale = 1.0 / math.sqrt(HD)
    slot_rows = recv_ref.shape[0] * recv_ref.shape[1]
    recv = recv_ref[...].reshape(slot_rows, recv_ref.shape[2])
    outs = []
    kv_heads = pool_ref.shape[1] // (2 * HD)
    q_width = kv_heads * QPK * HD
    table = table_ref[...]
    spread = jnp.broadcast_to(table[0:1, :], (HD, slot_rows))
    begins = jnp.transpose(spread)[:, 0:1]
    ends = begins + jnp.transpose(jnp.broadcast_to(table[1:2, :], (HD, slot_rows)))[:, 0:1]
    places = lax.broadcasted_iota(jnp.int32, (slot_rows, pool_ref.shape[0]), 1)
    visible = (places >= begins) & (places < ends)
    for g in range(kv_heads):
        keys = pool_ref[:, g * 2 * HD : g * 2 * HD + HD]
        vals = pool_ref[:, g * 2 * HD + HD : (g + 1) * 2 * HD]
        own_key = recv[:, q_width + g * 2 * HD : q_width + g * 2 * HD + HD].astype(jnp.float32)
        own_val = recv[:, q_width + g * 2 * HD + HD : q_width + (g + 1) * 2 * HD].astype(jnp.float32)
        for h in range(QPK):
            col = (g * QPK + h) * HD
            q = recv[:, col : col + HD]
            scores = lax.dot_general(
                q, keys, (((1,), (1,)), ((), ())), preferred_element_type=jnp.float32
            ) * score_scale
            scores = jnp.where(visible, scores, MASKED_SCORE)
            own = jnp.sum(q.astype(jnp.float32) * own_key, axis=1, keepdims=True) * score_scale
            peak = jnp.maximum(jnp.max(scores, axis=1, keepdims=True), own)
            weights = jnp.where(visible, jnp.exp(scores - peak), 0.0)
            own_exp = jnp.exp(own - peak)
            total = jnp.sum(weights, axis=1, keepdims=True) + own_exp
            weights = (weights / total).astype(jnp.bfloat16)
            own_weight = (own_exp / total).astype(jnp.bfloat16).astype(jnp.float32)
            mixed = jnp.dot(weights, vals, preferred_element_type=jnp.float32) + own_weight * own_val
            outs.append(mixed.astype(jnp.bfloat16))
    out_ref[...] = jnp.concatenate(outs, axis=1).reshape(out_ref.shape)


def prefill_kernel(q_ref, kv_ref, meta_ref, pool_ref, out_ref):
    score_scale = 1.0 / math.sqrt(HD)
    span_rows = q_ref.shape[0]
    pool_len = pool_ref.shape[0]
    kv_heads = pool_ref.shape[1] // (2 * HD)
    meta = meta_ref[...]
    begin = meta[:, 0:1]
    end = begin + meta[:, 1:2]
    places = lax.broadcasted_iota(jnp.int32, (span_rows, pool_len), 1)
    visible = (places >= begin) & (places < end)
    row_iota = lax.broadcasted_iota(jnp.int32, (span_rows, span_rows), 0)
    col_iota = lax.broadcasted_iota(jnp.int32, (span_rows, span_rows), 1)
    causal = col_iota <= row_iota
    live = lax.broadcasted_iota(jnp.int32, (span_rows, 1), 0) < meta[:, 2:3]
    for g in range(kv_heads):
        keys = pool_ref[:, g * 2 * HD : g * 2 * HD + HD]
        vals = pool_ref[:, g * 2 * HD + HD : (g + 1) * 2 * HD]
        span_keys = kv_ref[:, g * 2 * HD : g * 2 * HD + HD]
        span_vals = kv_ref[:, g * 2 * HD + HD : (g + 1) * 2 * HD]
        for h in range(QPK):
            col = (g * QPK + h) * HD
            q = q_ref[:, col : col + HD]
            dims = (((1,), (1,)), ((), ()))
            pool_scores = lax.dot_general(q, keys, dims, preferred_element_type=jnp.float32) * score_scale
            pool_scores = jnp.where(visible, pool_scores, MASKED_SCORE)
            span_scores = lax.dot_general(q, span_keys, dims, preferred_element_type=jnp.float32) * score_scale
            span_scores = jnp.where(causal, span_scores, MASKED_SCORE)
            peak = jnp.maximum(
                jnp.max(pool_scores, axis=1, keepdims=True), jnp.max(span_scores, axis=1, keepdims=True)
            )
            pool_exp = jnp.where(visible, jnp.exp(pool_scores - peak), 0.0)
            span_exp = jnp.where(causal, jnp.exp(span_scores - peak), 0.0)
            total = jnp.sum(pool_exp, axis=1, keepdims=True) + jnp.sum(span_exp, axis=1, keepdims=True)
            pool_weight = (pool_exp / total).astype(jnp.bfloat16)
            span_weight = (span_exp / total).astype(jnp.bfloat16)
            mixed = jnp.dot(pool_weight, vals, preferred_element_type=jnp.float32) + jnp.dot(
                span_weight, span_vals, preferred_element_type=jnp.float32
            )
            out_ref[:, col : col + HD] = jnp.where(live, mixed, 0.0).astype(jnp.bfloat16)


def route_kernel(owner_ref, q_ref, kv_ref, send_ref, dispatch_ref):
    tok_rows = q_ref.shape[0]
    slot_count = dispatch_ref.shape[0]
    capacity = slot_count // send_ref.shape[0]
    owner_row = owner_ref[...]
    owner_col = jnp.transpose(jnp.broadcast_to(owner_row, (tok_rows, tok_rows)))
    earlier = lax.broadcasted_iota(jnp.int32, (tok_rows, tok_rows), 0) < lax.broadcasted_iota(
        jnp.int32, (tok_rows, tok_rows), 1
    )
    same = (owner_col == owner_row) & earlier
    ranking = jnp.sum(same.astype(jnp.int32), axis=0, keepdims=True)
    slot_ids = owner_row * capacity + ranking
    slots = lax.broadcasted_iota(jnp.int32, (slot_count, tok_rows), 0)
    dispatch = (slots == slot_ids).astype(jnp.bfloat16)
    dispatch_ref[...] = dispatch
    rows = jnp.concatenate([q_ref[...], kv_ref[...]], axis=1)
    send = jnp.dot(dispatch, rows, preferred_element_type=jnp.float32).astype(jnp.bfloat16)
    send_ref[...] = send.reshape(send_ref.shape)


def vmem_call(kernel, out_shape, operands, flops, transcendentals):
    bytes_accessed = sum(x.size * x.dtype.itemsize for x in operands) + out_shape.size * 2
    return pl.pallas_call(
        kernel,
        out_shape=out_shape,
        in_specs=[pl.BlockSpec(memory_space=pltpu.VMEM)] * len(operands),
        out_specs=pl.BlockSpec(memory_space=pltpu.VMEM),
        cost_estimate=pl.CostEstimate(
            flops=flops, transcendentals=transcendentals, bytes_accessed=bytes_accessed
        ),
    )(*operands)


def term_maker(rows_source, wo):
    return jnp.dot(rows_source, wo, preferred_element_type=jnp.float32)


def per_device(dec_q, dec_kv, dec_owner, dec_table, pre_q, pre_kv, pre_meta, pool, wo):
    groups = lax.axis_size("req")
    tok_rows = dec_q.shape[0]
    capacity = max(2, (2 * tok_rows + groups - 1) // groups)
    slot_count = groups * capacity
    q_width = dec_q.shape[1]
    kv_width = dec_kv.shape[1]

    span_rows = pre_q.shape[0]
    pre_attn = vmem_call(
        prefill_kernel,
        jax.ShapeDtypeStruct((span_rows, q_width), jnp.bfloat16),
        (pre_q, pre_kv, pre_meta, pool),
        4 * span_rows * (pool.shape[0] + span_rows) * q_width,
        span_rows * (pool.shape[0] + span_rows) * q_width // HD,
    )
    pre_part = term_maker(pre_attn, wo).astype(jnp.bfloat16)

    send, dispatch = pl.pallas_call(
        route_kernel,
        out_shape=(
            jax.ShapeDtypeStruct((groups, capacity, q_width + kv_width), jnp.bfloat16),
            jax.ShapeDtypeStruct((slot_count, tok_rows), jnp.bfloat16),
        ),
        in_specs=[pl.BlockSpec(memory_space=pltpu.VMEM)] * 3,
        out_specs=(pl.BlockSpec(memory_space=pltpu.VMEM), pl.BlockSpec(memory_space=pltpu.VMEM)),
        cost_estimate=pl.CostEstimate(
            flops=2 * slot_count * tok_rows * (q_width + kv_width),
            transcendentals=0,
            bytes_accessed=2 * (tok_rows + slot_count) * (q_width + kv_width),
        ),
    )(dec_owner.reshape(1, tok_rows), dec_q, dec_kv)
    recv = lax.all_to_all(send, "req", split_axis=0, concat_axis=0, tiled=True)
    pre_part, recv = lax.optimization_barrier((pre_part, recv))
    pre_out = lax.psum_scatter(pre_part, "tp", scatter_dimension=0, tiled=True)
    slot_attn = vmem_call(
        decode_kernel,
        jax.ShapeDtypeStruct((groups, capacity, q_width), jnp.bfloat16),
        (pltpu.with_memory_space_constraint(recv, pltpu.VMEM), jnp.transpose(dec_table), pool),
        4 * slot_count * pool.shape[0] * q_width,
        slot_count * pool.shape[0] * q_width // HD,
    )
    replies = lax.all_to_all(slot_attn, "req", split_axis=0, concat_axis=0, tiled=True)
    dec_attn = lax.dot_general(
        dispatch,
        replies.reshape(slot_count, q_width),
        (((0,), (0,)), ((), ())),
        preferred_element_type=jnp.float32,
    ).astype(jnp.bfloat16)
    tp_count = lax.axis_size("tp")
    dec_part = term_maker(dec_attn, wo).astype(jnp.bfloat16)
    pieces = lax.all_to_all(
        dec_part.reshape(tp_count, tok_rows // tp_count, dec_part.shape[1]),
        "tp",
        split_axis=0,
        concat_axis=0,
        tiled=True,
    )
    dec_out = jnp.sum(pieces.astype(jnp.float32), axis=0).astype(jnp.bfloat16)
    return (dec_out, pre_out)


def solution(mesh):
    placed = (
        P("req", "tp"),
        P("req", "tp"),
        P("req"),
        P("req", None),
        P("req", "tp"),
        P("req", "tp"),
        P("req", None),
        P("req", "tp"),
        P("tp", None),
    )
    return jax.shard_map(
        per_device,
        mesh=mesh,
        in_specs=placed,
        out_specs=(P(("req", "tp"), None), P(("req", "tp"), None)),
        check_vma=False,
    )
```

```python
import math

import jax
import jax.numpy as jnp
from jax import lax
from jax.experimental import pallas as pl
from jax.experimental.pallas import tpu as pltpu
from jax.sharding import PartitionSpec as P

HD = 128
QPK = 3


MASKED_SCORE = -1e30


def decode_kernel(recv_ref, table_ref, pool_ref, out_ref):
    score_scale = 1.0 / math.sqrt(HD)
    slot_rows = recv_ref.shape[0] * recv_ref.shape[1]
    recv = recv_ref[...].reshape(slot_rows, recv_ref.shape[2])
    outs = []
    kv_heads = pool_ref.shape[1] // (2 * HD)
    q_width = kv_heads * QPK * HD
    table = table_ref[...]
    spread = jnp.broadcast_to(table[0:1, :], (HD, slot_rows))
    begins = jnp.transpose(spread)[:, 0:1]
    ends = begins + jnp.transpose(jnp.broadcast_to(table[1:2, :], (HD, slot_rows)))[:, 0:1]
    places = lax.broadcasted_iota(jnp.int32, (slot_rows, pool_ref.shape[0]), 1)
    visible = (places >= begins) & (places < ends)
    for g in range(kv_heads):
        keys = pool_ref[:, g * 2 * HD : g * 2 * HD + HD]
        vals = pool_ref[:, g * 2 * HD + HD : (g + 1) * 2 * HD]
        own_key = recv[:, q_width + g * 2 * HD : q_width + g * 2 * HD + HD].astype(jnp.float32)
        own_val = recv[:, q_width + g * 2 * HD + HD : q_width + (g + 1) * 2 * HD].astype(jnp.float32)
        for h in range(QPK):
            col = (g * QPK + h) * HD
            q = recv[:, col : col + HD]
            scores = lax.dot_general(
                q, keys, (((1,), (1,)), ((), ())), preferred_element_type=jnp.float32
            ) * score_scale
            scores = jnp.where(visible, scores, MASKED_SCORE)
            own = jnp.sum(q.astype(jnp.float32) * own_key, axis=1, keepdims=True) * score_scale
            peak = jnp.maximum(jnp.max(scores, axis=1, keepdims=True), own)
            weights = jnp.where(visible, jnp.exp(scores - peak), 0.0)
            own_exp = jnp.exp(own - peak)
            total = jnp.sum(weights, axis=1, keepdims=True) + own_exp
            weights = (weights / total).astype(jnp.bfloat16)
            own_weight = (own_exp / total).astype(jnp.bfloat16).astype(jnp.float32)
            mixed = jnp.dot(weights, vals, preferred_element_type=jnp.float32) + own_weight * own_val
            outs.append(mixed.astype(jnp.bfloat16))
    out_ref[...] = jnp.concatenate(outs, axis=1).reshape(out_ref.shape)


def prefill_kernel(q_ref, kv_ref, meta_ref, pool_ref, out_ref):
    score_scale = 1.0 / math.sqrt(HD)
    span_rows = q_ref.shape[0]
    pool_len = pool_ref.shape[0]
    kv_heads = pool_ref.shape[1] // (2 * HD)
    meta = meta_ref[...]
    begin = meta[:, 0:1]
    end = begin + meta[:, 1:2]
    places = lax.broadcasted_iota(jnp.int32, (span_rows, pool_len), 1)
    visible = (places >= begin) & (places < end)
    row_iota = lax.broadcasted_iota(jnp.int32, (span_rows, span_rows), 0)
    col_iota = lax.broadcasted_iota(jnp.int32, (span_rows, span_rows), 1)
    causal = col_iota <= row_iota
    live = lax.broadcasted_iota(jnp.int32, (span_rows, 1), 0) < meta[:, 2:3]
    for g in range(kv_heads):
        keys = pool_ref[:, g * 2 * HD : g * 2 * HD + HD]
        vals = pool_ref[:, g * 2 * HD + HD : (g + 1) * 2 * HD]
        span_keys = kv_ref[:, g * 2 * HD : g * 2 * HD + HD]
        span_vals = kv_ref[:, g * 2 * HD + HD : (g + 1) * 2 * HD]
        for h in range(QPK):
            col = (g * QPK + h) * HD
            q = q_ref[:, col : col + HD]
            dims = (((1,), (1,)), ((), ()))
            pool_scores = lax.dot_general(q, keys, dims, preferred_element_type=jnp.float32) * score_scale
            pool_scores = jnp.where(visible, pool_scores, MASKED_SCORE)
            span_scores = lax.dot_general(q, span_keys, dims, preferred_element_type=jnp.float32) * score_scale
            span_scores = jnp.where(causal, span_scores, MASKED_SCORE)
            peak = jnp.maximum(
                jnp.max(pool_scores, axis=1, keepdims=True), jnp.max(span_scores, axis=1, keepdims=True)
            )
            pool_exp = jnp.where(visible, jnp.exp(pool_scores - peak), 0.0)
            span_exp = jnp.where(causal, jnp.exp(span_scores - peak), 0.0)
            total = jnp.sum(pool_exp, axis=1, keepdims=True) + jnp.sum(span_exp, axis=1, keepdims=True)
            pool_weight = (pool_exp / total).astype(jnp.bfloat16)
            span_weight = (span_exp / total).astype(jnp.bfloat16)
            mixed = jnp.dot(pool_weight, vals, preferred_element_type=jnp.float32) + jnp.dot(
                span_weight, span_vals, preferred_element_type=jnp.float32
            )
            out_ref[:, col : col + HD] = jnp.where(live, mixed, 0.0).astype(jnp.bfloat16)


def route_kernel(owner_ref, q_ref, kv_ref, send_ref):
    tok_rows = q_ref.shape[0]
    capacity = send_ref.shape[1]
    slot_count = send_ref.shape[0] * capacity
    owner_row = owner_ref[...]
    owner_col = jnp.transpose(jnp.broadcast_to(owner_row, (tok_rows, tok_rows)))
    earlier = lax.broadcasted_iota(jnp.int32, (tok_rows, tok_rows), 0) < lax.broadcasted_iota(
        jnp.int32, (tok_rows, tok_rows), 1
    )
    same = (owner_col == owner_row) & earlier
    ranking = jnp.sum(same.astype(jnp.int32), axis=0, keepdims=True)
    slot_ids = owner_row * capacity + ranking
    slots = lax.broadcasted_iota(jnp.int32, (slot_count, tok_rows), 0)
    dispatch = (slots == slot_ids).astype(jnp.bfloat16)
    rows = jnp.concatenate([q_ref[...], kv_ref[...]], axis=1)
    send = jnp.dot(dispatch, rows, preferred_element_type=jnp.float32).astype(jnp.bfloat16)
    send_ref[...] = send.reshape(send_ref.shape)


def vmem_call(kernel, out_shape, operands, flops, transcendentals):
    bytes_accessed = sum(x.size * x.dtype.itemsize for x in operands) + out_shape.size * 2
    return pl.pallas_call(
        kernel,
        out_shape=out_shape,
        in_specs=[pl.BlockSpec(memory_space=pltpu.VMEM)] * len(operands),
        out_specs=pl.BlockSpec(memory_space=pltpu.VMEM),
        cost_estimate=pl.CostEstimate(
            flops=flops, transcendentals=transcendentals, bytes_accessed=bytes_accessed
        ),
    )(*operands)


def term_maker(rows_source, wo):
    return jnp.dot(rows_source, wo, preferred_element_type=jnp.float32)


def per_device(dec_q, dec_kv, dec_owner, dec_table, pre_q, pre_kv, pre_meta, pool, wo):
    groups = lax.axis_size("req")
    tok_rows = dec_q.shape[0]
    capacity = max(2, (2 * tok_rows + groups - 1) // groups)
    slot_count = groups * capacity
    q_width = dec_q.shape[1]
    kv_width = dec_kv.shape[1]

    span_rows = pre_q.shape[0]
    pre_attn = vmem_call(
        prefill_kernel,
        jax.ShapeDtypeStruct((span_rows, q_width), jnp.bfloat16),
        (pre_q, pre_kv, pre_meta, pool),
        4 * span_rows * (pool.shape[0] + span_rows) * q_width,
        span_rows * (pool.shape[0] + span_rows) * q_width // HD,
    )
    pre_part = term_maker(pre_attn, wo).astype(jnp.bfloat16)

    send = pl.pallas_call(
        route_kernel,
        out_shape=jax.ShapeDtypeStruct((groups, capacity, q_width + kv_width), jnp.bfloat16),
        in_specs=[pl.BlockSpec(memory_space=pltpu.VMEM)] * 3,
        out_specs=pl.BlockSpec(memory_space=pltpu.VMEM),
        cost_estimate=pl.CostEstimate(
            flops=2 * slot_count * tok_rows * (q_width + kv_width),
            transcendentals=0,
            bytes_accessed=2 * (tok_rows + slot_count) * (q_width + kv_width),
        ),
    )(dec_owner.reshape(1, tok_rows), dec_q, dec_kv)
    tok_iota = lax.iota(jnp.int32, tok_rows)
    earlier_same = (dec_owner[:, None] == dec_owner[None, :]) & (tok_iota[None, :] < tok_iota[:, None])
    slot_ids = dec_owner * capacity + jnp.sum(earlier_same.astype(jnp.int32), axis=1)
    dispatch = (slot_ids[None, :] == lax.iota(jnp.int32, slot_count)[:, None]).astype(jnp.bfloat16)
    recv = lax.all_to_all(send, "req", split_axis=0, concat_axis=0, tiled=True)
    pre_part, recv = lax.optimization_barrier((pre_part, recv))
    pre_out = lax.psum_scatter(pre_part, "tp", scatter_dimension=0, tiled=True)
    slot_attn = vmem_call(
        decode_kernel,
        jax.ShapeDtypeStruct((groups, capacity, q_width), jnp.bfloat16),
        (recv, jnp.transpose(dec_table), pool),
        4 * slot_count * pool.shape[0] * q_width,
        slot_count * pool.shape[0] * q_width // HD,
    )
    replies = lax.all_to_all(slot_attn, "req", split_axis=0, concat_axis=0, tiled=True)
    dec_attn = lax.dot_general(
        dispatch,
        replies.reshape(slot_count, q_width),
        (((0,), (0,)), ((), ())),
        preferred_element_type=jnp.float32,
    ).astype(jnp.bfloat16)
    tp_count = lax.axis_size("tp")
    dec_part = term_maker(dec_attn, wo).astype(jnp.bfloat16)
    pieces = lax.all_to_all(
        dec_part.reshape(tp_count, tok_rows // tp_count, dec_part.shape[1]),
        "tp",
        split_axis=0,
        concat_axis=0,
        tiled=True,
    )
    dec_out = jnp.sum(pieces.astype(jnp.float32), axis=0).astype(jnp.bfloat16)
    return (dec_out, pre_out)


def solution(mesh):
    placed = (
        P("req", "tp"),
        P("req", "tp"),
        P("req"),
        P("req", None),
        P("req", "tp"),
        P("req", "tp"),
        P("req", None),
        P("req", "tp"),
        P("tp", None),
    )
    return jax.shard_map(
        per_device,
        mesh=mesh,
        in_specs=placed,
        out_specs=(P(("req", "tp"), None), P(("req", "tp"), None)),
        check_vma=False,
    )
```

```python
import math

import jax
import jax.numpy as jnp
from jax import lax
from jax.experimental import pallas as pl
from jax.experimental.pallas import tpu as pltpu
from jax.sharding import PartitionSpec as P

HD = 128
QPK = 3


MASKED_SCORE = -1e30


def decode_kernel(recv_ref, table_ref, pool_ref, out_ref):
    score_scale = 1.0 / math.sqrt(HD)
    slot_rows = recv_ref.shape[0] * recv_ref.shape[1]
    recv = recv_ref[...].reshape(slot_rows, recv_ref.shape[2])
    outs = []
    kv_heads = pool_ref.shape[1] // (2 * HD)
    q_width = kv_heads * QPK * HD
    table = table_ref[...]
    spread = jnp.broadcast_to(table[0:1, :], (HD, slot_rows))
    begins = jnp.transpose(spread)[:, 0:1]
    ends = begins + jnp.transpose(jnp.broadcast_to(table[1:2, :], (HD, slot_rows)))[:, 0:1]
    places = lax.broadcasted_iota(jnp.int32, (slot_rows, pool_ref.shape[0]), 1)
    visible = (places >= begins) & (places < ends)
    for g in range(kv_heads):
        keys = pool_ref[:, g * 2 * HD : g * 2 * HD + HD]
        vals = pool_ref[:, g * 2 * HD + HD : (g + 1) * 2 * HD]
        own_key = recv[:, q_width + g * 2 * HD : q_width + g * 2 * HD + HD].astype(jnp.float32)
        own_val = recv[:, q_width + g * 2 * HD + HD : q_width + (g + 1) * 2 * HD].astype(jnp.float32)
        for h in range(QPK):
            col = (g * QPK + h) * HD
            q = recv[:, col : col + HD]
            scores = lax.dot_general(
                q, keys, (((1,), (1,)), ((), ())), preferred_element_type=jnp.float32
            ) * score_scale
            scores = jnp.where(visible, scores, MASKED_SCORE)
            own = jnp.sum(q.astype(jnp.float32) * own_key, axis=1, keepdims=True) * score_scale
            peak = jnp.maximum(jnp.max(scores, axis=1, keepdims=True), own)
            weights = jnp.where(visible, jnp.exp(scores - peak), 0.0)
            own_exp = jnp.exp(own - peak)
            total = jnp.sum(weights, axis=1, keepdims=True) + own_exp
            weights = (weights / total).astype(jnp.bfloat16)
            own_weight = (own_exp / total).astype(jnp.bfloat16).astype(jnp.float32)
            mixed = jnp.dot(weights, vals, preferred_element_type=jnp.float32) + own_weight * own_val
            outs.append(mixed.astype(jnp.bfloat16))
    out_ref[...] = jnp.concatenate(outs, axis=1).reshape(out_ref.shape)


def prefill_kernel(q_ref, kv_ref, meta_ref, pool_ref, out_ref):
    score_scale = 1.0 / math.sqrt(HD)
    span_rows = q_ref.shape[0]
    pool_len = pool_ref.shape[0]
    kv_heads = pool_ref.shape[1] // (2 * HD)
    meta = meta_ref[...]
    begin = meta[:, 0:1]
    end = begin + meta[:, 1:2]
    places = lax.broadcasted_iota(jnp.int32, (span_rows, pool_len), 1)
    visible = (places >= begin) & (places < end)
    row_iota = lax.broadcasted_iota(jnp.int32, (span_rows, span_rows), 0)
    col_iota = lax.broadcasted_iota(jnp.int32, (span_rows, span_rows), 1)
    causal = col_iota <= row_iota
    live = lax.broadcasted_iota(jnp.int32, (span_rows, 1), 0) < meta[:, 2:3]
    for g in range(kv_heads):
        keys = pool_ref[:, g * 2 * HD : g * 2 * HD + HD]
        vals = pool_ref[:, g * 2 * HD + HD : (g + 1) * 2 * HD]
        span_keys = kv_ref[:, g * 2 * HD : g * 2 * HD + HD]
        span_vals = kv_ref[:, g * 2 * HD + HD : (g + 1) * 2 * HD]
        for h in range(QPK):
            col = (g * QPK + h) * HD
            q = q_ref[:, col : col + HD]
            dims = (((1,), (1,)), ((), ()))
            pool_scores = lax.dot_general(q, keys, dims, preferred_element_type=jnp.float32) * score_scale
            pool_scores = jnp.where(visible, pool_scores, MASKED_SCORE)
            span_scores = lax.dot_general(q, span_keys, dims, preferred_element_type=jnp.float32) * score_scale
            span_scores = jnp.where(causal, span_scores, MASKED_SCORE)
            peak = jnp.maximum(
                jnp.max(pool_scores, axis=1, keepdims=True), jnp.max(span_scores, axis=1, keepdims=True)
            )
            pool_exp = jnp.where(visible, jnp.exp(pool_scores - peak), 0.0)
            span_exp = jnp.where(causal, jnp.exp(span_scores - peak), 0.0)
            total = jnp.sum(pool_exp, axis=1, keepdims=True) + jnp.sum(span_exp, axis=1, keepdims=True)
            pool_weight = (pool_exp / total).astype(jnp.bfloat16)
            span_weight = (span_exp / total).astype(jnp.bfloat16)
            mixed = jnp.dot(pool_weight, vals, preferred_element_type=jnp.float32) + jnp.dot(
                span_weight, span_vals, preferred_element_type=jnp.float32
            )
            out_ref[:, col : col + HD] = jnp.where(live, mixed, 0.0).astype(jnp.bfloat16)


def route_kernel(owner_ref, q_ref, kv_ref, send_ref, dispatch_ref):
    tok_rows = q_ref.shape[0]
    slot_count = dispatch_ref.shape[0]
    capacity = slot_count // send_ref.shape[0]
    owner_row = owner_ref[...]
    owner_col = jnp.transpose(jnp.broadcast_to(owner_row, (tok_rows, tok_rows)))
    earlier = lax.broadcasted_iota(jnp.int32, (tok_rows, tok_rows), 0) < lax.broadcasted_iota(
        jnp.int32, (tok_rows, tok_rows), 1
    )
    same = (owner_col == owner_row) & earlier
    ranking = jnp.sum(same.astype(jnp.int32), axis=0, keepdims=True)
    slot_ids = owner_row * capacity + ranking
    slots = lax.broadcasted_iota(jnp.int32, (slot_count, tok_rows), 0)
    dispatch = (slots == slot_ids).astype(jnp.bfloat16)
    dispatch_ref[...] = dispatch
    rows = jnp.concatenate([q_ref[...], kv_ref[...]], axis=1)
    send = jnp.dot(dispatch, rows, preferred_element_type=jnp.float32).astype(jnp.bfloat16)
    send_ref[...] = send.reshape(send_ref.shape)


def vmem_call(kernel, out_shape, operands, flops, transcendentals):
    bytes_accessed = sum(x.size * x.dtype.itemsize for x in operands) + out_shape.size * 2
    return pl.pallas_call(
        kernel,
        out_shape=out_shape,
        in_specs=[pl.BlockSpec(memory_space=pltpu.VMEM)] * len(operands),
        out_specs=pl.BlockSpec(memory_space=pltpu.VMEM),
        cost_estimate=pl.CostEstimate(
            flops=flops, transcendentals=transcendentals, bytes_accessed=bytes_accessed
        ),
    )(*operands)


def term_maker(rows_source, wo):
    return jnp.dot(rows_source, wo, preferred_element_type=jnp.float32)


def per_device(dec_q, dec_kv, dec_owner, dec_table, pre_q, pre_kv, pre_meta, pool, wo):
    groups = lax.axis_size("req")
    tok_rows = dec_q.shape[0]
    capacity = max(2, (2 * tok_rows + groups - 1) // groups)
    slot_count = groups * capacity
    q_width = dec_q.shape[1]
    kv_width = dec_kv.shape[1]

    span_rows = pre_q.shape[0]
    pre_attn = vmem_call(
        prefill_kernel,
        jax.ShapeDtypeStruct((span_rows, q_width), jnp.bfloat16),
        (pre_q, pre_kv, pre_meta, pool),
        4 * span_rows * (pool.shape[0] + span_rows) * q_width,
        span_rows * (pool.shape[0] + span_rows) * q_width // HD,
    )
    pre_part = term_maker(pre_attn, wo).astype(jnp.bfloat16)

    send, dispatch = pl.pallas_call(
        route_kernel,
        out_shape=(
            jax.ShapeDtypeStruct((groups, capacity, q_width + kv_width), jnp.bfloat16),
            jax.ShapeDtypeStruct((slot_count, tok_rows), jnp.bfloat16),
        ),
        in_specs=[pl.BlockSpec(memory_space=pltpu.VMEM)] * 3,
        out_specs=(pl.BlockSpec(memory_space=pltpu.VMEM), pl.BlockSpec(memory_space=pltpu.VMEM)),
        cost_estimate=pl.CostEstimate(
            flops=2 * slot_count * tok_rows * (q_width + kv_width),
            transcendentals=0,
            bytes_accessed=2 * (tok_rows + slot_count) * (q_width + kv_width),
        ),
    )(dec_owner.reshape(1, tok_rows), dec_q, dec_kv)
    recv = lax.all_to_all(send, "req", split_axis=0, concat_axis=0, tiled=True)
    pre_part, recv = lax.optimization_barrier((pre_part, recv))
    pre_out = lax.psum_scatter(pre_part, ("tpa", "tpb"), scatter_dimension=0, tiled=True)
    slot_attn = vmem_call(
        decode_kernel,
        jax.ShapeDtypeStruct((groups, capacity, q_width), jnp.bfloat16),
        (recv, jnp.transpose(dec_table), pool),
        4 * slot_count * pool.shape[0] * q_width,
        slot_count * pool.shape[0] * q_width // HD,
    )
    replies = lax.all_to_all(slot_attn, "req", split_axis=0, concat_axis=0, tiled=True)
    dec_attn = lax.dot_general(
        dispatch,
        replies.reshape(slot_count, q_width),
        (((0,), (0,)), ((), ())),
        preferred_element_type=jnp.float32,
    ).astype(jnp.bfloat16)
    tp_count = lax.axis_size(("tpa", "tpb"))
    dec_part = term_maker(dec_attn, wo).astype(jnp.bfloat16)
    outer = lax.axis_size("tpa")
    inner = lax.axis_size("tpb")
    chunks = dec_part.reshape(outer, inner, tok_rows // tp_count, dec_part.shape[1])
    me_inner = lax.axis_index("tpb")
    kept = lax.dynamic_index_in_dim(chunks, me_inner, 1, keepdims=False)
    given = lax.dynamic_index_in_dim(chunks, (me_inner + 1) % inner, 1, keepdims=False)
    got = lax.ppermute(given, "tpb", [(i, (i + 1) % inner) for i in range(inner)])
    pair = (kept.astype(jnp.float32) + got.astype(jnp.float32)).astype(jnp.bfloat16)
    pieces = lax.all_to_all(pair, "tpa", split_axis=0, concat_axis=0, tiled=True)
    dec_out = jnp.sum(pieces.astype(jnp.float32), axis=0).astype(jnp.bfloat16)
    return (dec_out, pre_out)


def solution(mesh):
    n_tp = mesh.shape["tp"]
    split = jax.sharding.Mesh(
        mesh.devices.reshape(mesh.shape["req"], n_tp // 2, 2), ("req", "tpa", "tpb")
    )
    tp = ("tpa", "tpb")
    placed = (
        P("req", tp),
        P("req", tp),
        P("req"),
        P("req", None),
        P("req", tp),
        P("req", tp),
        P("req", None),
        P("req", tp),
        P(tp, None),
    )
    return jax.shard_map(
        per_device,
        mesh=split,
        in_specs=placed,
        out_specs=(P(("req",) + tp, None), P(("req",) + tp, None)),
        check_vma=False,
    )
```

```python
import math

import jax
import jax.numpy as jnp
from jax import lax
from jax.experimental import pallas as pl
from jax.experimental.pallas import tpu as pltpu
from jax.sharding import PartitionSpec as P

HD = 128
QPK = 3


MASKED_SCORE = -1e30


def decode_kernel(recv_ref, table_ref, pool_ref, out_ref):
    score_scale = 1.0 / math.sqrt(HD)
    slot_rows = recv_ref.shape[0] * recv_ref.shape[1]
    recv = recv_ref[...].reshape(slot_rows, recv_ref.shape[2])
    outs = []
    kv_heads = pool_ref.shape[1] // (2 * HD)
    q_width = kv_heads * QPK * HD
    table = table_ref[...]
    spread = jnp.broadcast_to(table[0:1, :], (HD, slot_rows))
    begins = jnp.transpose(spread)[:, 0:1]
    ends = begins + jnp.transpose(jnp.broadcast_to(table[1:2, :], (HD, slot_rows)))[:, 0:1]
    places = lax.broadcasted_iota(jnp.int32, (slot_rows, pool_ref.shape[0]), 1)
    visible = (places >= begins) & (places < ends)
    for g in range(kv_heads):
        keys = pool_ref[:, g * 2 * HD : g * 2 * HD + HD]
        vals = pool_ref[:, g * 2 * HD + HD : (g + 1) * 2 * HD]
        own_key = recv[:, q_width + g * 2 * HD : q_width + g * 2 * HD + HD].astype(jnp.float32)
        own_val = recv[:, q_width + g * 2 * HD + HD : q_width + (g + 1) * 2 * HD].astype(jnp.float32)
        for h in range(QPK):
            col = (g * QPK + h) * HD
            q = recv[:, col : col + HD]
            scores = lax.dot_general(
                q, keys, (((1,), (1,)), ((), ())), preferred_element_type=jnp.float32
            ) * score_scale
            scores = jnp.where(visible, scores, MASKED_SCORE)
            own = jnp.sum(q.astype(jnp.float32) * own_key, axis=1, keepdims=True) * score_scale
            peak = jnp.maximum(jnp.max(scores, axis=1, keepdims=True), own)
            weights = jnp.where(visible, jnp.exp(scores - peak), 0.0)
            own_exp = jnp.exp(own - peak)
            total = jnp.sum(weights, axis=1, keepdims=True) + own_exp
            weights = (weights / total).astype(jnp.bfloat16)
            own_weight = (own_exp / total).astype(jnp.bfloat16).astype(jnp.float32)
            mixed = jnp.dot(weights, vals, preferred_element_type=jnp.float32) + own_weight * own_val
            outs.append(mixed.astype(jnp.bfloat16))
    out_ref[...] = jnp.concatenate(outs, axis=1).reshape(out_ref.shape)


def prefill_kernel(q_ref, kv_ref, meta_ref, pool_ref, out_ref):
    score_scale = 1.0 / math.sqrt(HD)
    span_rows = q_ref.shape[0]
    pool_len = pool_ref.shape[0]
    kv_heads = pool_ref.shape[1] // (2 * HD)
    meta = meta_ref[...]
    begin = meta[:, 0:1]
    end = begin + meta[:, 1:2]
    places = lax.broadcasted_iota(jnp.int32, (span_rows, pool_len), 1)
    visible = (places >= begin) & (places < end)
    row_iota = lax.broadcasted_iota(jnp.int32, (span_rows, span_rows), 0)
    col_iota = lax.broadcasted_iota(jnp.int32, (span_rows, span_rows), 1)
    causal = col_iota <= row_iota
    live = lax.broadcasted_iota(jnp.int32, (span_rows, 1), 0) < meta[:, 2:3]
    for g in range(kv_heads):
        keys = pool_ref[:, g * 2 * HD : g * 2 * HD + HD]
        vals = pool_ref[:, g * 2 * HD + HD : (g + 1) * 2 * HD]
        span_keys = kv_ref[:, g * 2 * HD : g * 2 * HD + HD]
        span_vals = kv_ref[:, g * 2 * HD + HD : (g + 1) * 2 * HD]
        for h in range(QPK):
            col = (g * QPK + h) * HD
            q = q_ref[:, col : col + HD]
            dims = (((1,), (1,)), ((), ()))
            pool_scores = lax.dot_general(q, keys, dims, preferred_element_type=jnp.float32) * score_scale
            pool_scores = jnp.where(visible, pool_scores, MASKED_SCORE)
            span_scores = lax.dot_general(q, span_keys, dims, preferred_element_type=jnp.float32) * score_scale
            span_scores = jnp.where(causal, span_scores, MASKED_SCORE)
            peak = jnp.maximum(
                jnp.max(pool_scores, axis=1, keepdims=True), jnp.max(span_scores, axis=1, keepdims=True)
            )
            pool_exp = jnp.where(visible, jnp.exp(pool_scores - peak), 0.0)
            span_exp = jnp.where(causal, jnp.exp(span_scores - peak), 0.0)
            total = jnp.sum(pool_exp, axis=1, keepdims=True) + jnp.sum(span_exp, axis=1, keepdims=True)
            pool_weight = (pool_exp / total).astype(jnp.bfloat16)
            span_weight = (span_exp / total).astype(jnp.bfloat16)
            mixed = jnp.dot(pool_weight, vals, preferred_element_type=jnp.float32) + jnp.dot(
                span_weight, span_vals, preferred_element_type=jnp.float32
            )
            out_ref[:, col : col + HD] = jnp.where(live, mixed, 0.0).astype(jnp.bfloat16)


def route_kernel(owner_ref, q_ref, kv_ref, send_ref):
    tok_rows = q_ref.shape[0]
    capacity = send_ref.shape[1]
    slot_count = send_ref.shape[0] * capacity
    owner_row = owner_ref[...]
    owner_col = jnp.transpose(jnp.broadcast_to(owner_row, (tok_rows, tok_rows)))
    earlier = lax.broadcasted_iota(jnp.int32, (tok_rows, tok_rows), 0) < lax.broadcasted_iota(
        jnp.int32, (tok_rows, tok_rows), 1
    )
    same = (owner_col == owner_row) & earlier
    ranking = jnp.sum(same.astype(jnp.int32), axis=0, keepdims=True)
    slot_ids = owner_row * capacity + ranking
    slots = lax.broadcasted_iota(jnp.int32, (slot_count, tok_rows), 0)
    dispatch = (slots == slot_ids).astype(jnp.bfloat16)
    rows = jnp.concatenate([q_ref[...], kv_ref[...]], axis=1)
    send = jnp.dot(dispatch, rows, preferred_element_type=jnp.float32).astype(jnp.bfloat16)
    send_ref[...] = send.reshape(send_ref.shape)


def vmem_call(kernel, out_shape, operands, flops, transcendentals):
    bytes_accessed = sum(x.size * x.dtype.itemsize for x in operands) + out_shape.size * 2
    return pl.pallas_call(
        kernel,
        out_shape=out_shape,
        in_specs=[pl.BlockSpec(memory_space=pltpu.VMEM)] * len(operands),
        out_specs=pl.BlockSpec(memory_space=pltpu.VMEM),
        cost_estimate=pl.CostEstimate(
            flops=flops, transcendentals=transcendentals, bytes_accessed=bytes_accessed
        ),
    )(*operands)


def term_maker(rows_source, wo):
    return jnp.dot(rows_source, wo, preferred_element_type=jnp.float32)


def per_device(dec_q, dec_kv, dec_owner, dec_table, pre_q, pre_kv, pre_meta, pool, wo):
    groups = lax.axis_size("req")
    tok_rows = dec_q.shape[0]
    capacity = max(2, (2 * tok_rows + groups - 1) // groups)
    slot_count = groups * capacity
    q_width = dec_q.shape[1]
    kv_width = dec_kv.shape[1]

    span_rows = pre_q.shape[0]
    pre_attn = vmem_call(
        prefill_kernel,
        jax.ShapeDtypeStruct((span_rows, q_width), jnp.bfloat16),
        (pre_q, pre_kv, pre_meta, pool),
        4 * span_rows * (pool.shape[0] + span_rows) * q_width,
        span_rows * (pool.shape[0] + span_rows) * q_width // HD,
    )
    pre_part = term_maker(pre_attn, wo).astype(jnp.bfloat16)

    send = pl.pallas_call(
        route_kernel,
        out_shape=jax.ShapeDtypeStruct((groups, capacity, q_width + kv_width), jnp.bfloat16),
        in_specs=[pl.BlockSpec(memory_space=pltpu.VMEM)] * 3,
        out_specs=pl.BlockSpec(memory_space=pltpu.VMEM),
        cost_estimate=pl.CostEstimate(
            flops=2 * slot_count * tok_rows * (q_width + kv_width),
            transcendentals=0,
            bytes_accessed=2 * (tok_rows + slot_count) * (q_width + kv_width),
        ),
    )(dec_owner.reshape(1, tok_rows), dec_q, dec_kv)
    tok_iota = lax.iota(jnp.int32, tok_rows)
    earlier_same = (dec_owner[:, None] == dec_owner[None, :]) & (tok_iota[None, :] < tok_iota[:, None])
    slot_ids = dec_owner * capacity + jnp.sum(earlier_same.astype(jnp.int32), axis=1)
    dispatch = (slot_ids[None, :] == lax.iota(jnp.int32, slot_count)[:, None]).astype(jnp.bfloat16)
    recv = lax.all_to_all(send, "req", split_axis=0, concat_axis=0, tiled=True)
    pre_part, recv = lax.optimization_barrier((pre_part, recv))
    pre_out = lax.psum_scatter(pre_part, "tp", scatter_dimension=0, tiled=True)
    slot_attn = vmem_call(
        decode_kernel,
        jax.ShapeDtypeStruct((groups, capacity, q_width), jnp.bfloat16),
        (pltpu.with_memory_space_constraint(recv, pltpu.VMEM), jnp.transpose(dec_table), pool),
        4 * slot_count * pool.shape[0] * q_width,
        slot_count * pool.shape[0] * q_width // HD,
    )
    replies = lax.all_to_all(slot_attn, "req", split_axis=0, concat_axis=0, tiled=True)
    dec_attn = lax.dot_general(
        dispatch,
        replies.reshape(slot_count, q_width),
        (((0,), (0,)), ((), ())),
        preferred_element_type=jnp.float32,
    ).astype(jnp.bfloat16)
    tp_count = lax.axis_size("tp")
    dec_part = term_maker(dec_attn, wo).astype(jnp.bfloat16)
    pieces = lax.all_to_all(
        dec_part.reshape(tp_count, tok_rows // tp_count, dec_part.shape[1]),
        "tp",
        split_axis=0,
        concat_axis=0,
        tiled=True,
    )
    dec_out = jnp.sum(pieces.astype(jnp.float32), axis=0).astype(jnp.bfloat16)
    return (dec_out, pre_out)


def solution(mesh):
    placed = (
        P("req", "tp"),
        P("req", "tp"),
        P("req"),
        P("req", None),
        P("req", "tp"),
        P("req", "tp"),
        P("req", None),
        P("req", "tp"),
        P("tp", None),
    )
    return jax.shard_map(
        per_device,
        mesh=mesh,
        in_specs=placed,
        out_specs=(P(("req", "tp"), None), P(("req", "tp"), None)),
        check_vma=False,
    )
```
